32 devices in a mesh: ctx: 16 (over z, y, x), tp: 2 (over core).
Axes of the slice: x: 2, y: 2, z: 4, core: 2. Of those that a mesh axis runs over, the one named last changes fastest.
Arguments:
- tokens: bfloat16 [12288, 4096], P('ctx', 'tp'), may hold values from -6 to 6
- norm_gain: float32 [4096], replicated, may hold values from 0.1 to 1.9
- w_in: bfloat16 [4096, 3, 4096], P('ctx', None, 'tp'), may hold values from -0.09375 to 0.09375
- short_filter: float32 [3, 3, 4096], P(None, None, 'tp'), may hold values from -3.5 to 3.5
- long_filter: bfloat16 [128, 256], P(None, 'tp'), may hold values from -0.5 to 0.5
- w_out: bfloat16 [4096, 4096], P('tp', 'ctx'), may hold values from -0.125 to 0.125
Outputs:
- block_out: bfloat16 [12288, 4096], P('ctx', 'tp')
The draws below stay inside these ranges and needn't reach their ends.
All inputs are finite; a program needn't handle non-finite values.
Results may differ from the reference program's by a relative error of at most 0.008.
Values may be sent and summed in bfloat16 or wider, within the bound.
No kernel may reach another device: no remote copies, remote signals or barrier semaphores. Data moves between devices by JAX's collectives and lax.ppermute only.
A program may use at most 192 MiB of HBM per device.

```python
import jax
import jax.numpy as jnp
from jax import lax

D = 4096
KS = 3
KL = 128
GS = 16
TOKENS = 12288
G = 256
N_TP = 2


def with_spikes(drawn, rng, source, target, parts, factor):
    owner, partner = [(jnp.arange(drawn.shape[dim]) // (drawn.shape[dim] // parts)).reshape([-1 if axis == dim else 1 for axis in range(drawn.ndim)]) for dim in (source, target)]
    chosen = jax.random.permutation(rng, parts)[partner]
    strong = (owner == chosen) | (owner == (partner + parts // 2) % parts)
    return jnp.where(strong, factor * drawn, drawn)


def block_levels(own_key, extent, pieces, least, high):
    loudness, own = 1.0, jax.random.fold_in(own_key, 6)
    for position, shards_of in pieces:
        draws = jnp.exp(jax.random.uniform(jax.random.fold_in(own, position), (shards_of,), jnp.float32, least / len(pieces), high / len(pieces)))
        loudness = loudness * jnp.repeat(draws, extent[position] // shards_of).reshape([-1 if axis == position else 1 for axis in range(len(extent))])
    return loudness


def gaussian(own_key, shape, spread, limit, pieces=(), dtype=jnp.bfloat16):
    result = jax.random.normal(own_key, shape, jnp.float32) * spread
    if len(pieces) > 0:
        result = block_levels(own_key, shape, pieces, -0.22, 0.18) * result
    return jnp.clip(result, min=-limit, max=limit).astype(dtype)


def gaussian_with(key, dims, spread, bound, shards, heavy, kind=jnp.bfloat16):
    result = spread * jax.random.normal(key, dims, jnp.float32)
    if shards:
        result = result * block_levels(key, dims, shards, -0.22, 0.18)
    return jnp.clip(with_spikes(result, jax.random.fold_in(key, 3), *heavy), -bound, bound).astype(kind)


def setup_inputs(seed: int = 0) -> dict:
    keys = jax.random.split(jax.random.key(seed), 7)
    tokens = gaussian(keys[0], (TOKENS, D), 1.0, 6.0, ((0, 16), (1, 2)))
    norm_gain = jnp.clip(1.0 + 0.18 * jax.random.normal(keys[1], (D,), jnp.float32), 0.1, 1.9)
    w_in = gaussian(keys[2], (D, 3, D), D ** -0.5, 0.09375, ((0, 16), (2, 2)))
    short_filter = gaussian(keys[3], (KS, 3, D), KS ** -0.5, 3.5, ((2, 2),), jnp.float32)
    long_filter = gaussian(keys[4], (KL, G), KL ** -0.5, 0.5, ((1, 2),))
    w_out = gaussian_with(keys[5], (D, D), D ** -0.5, 0.125, ((0, 2), (1, 16)), (0, 1, 16, 2.0))
    return {"tokens": tokens, "norm_gain": norm_gain, "w_in": w_in, "short_filter": short_filter, "long_filter": long_filter, "w_out": w_out}


def toeplitz_pair(long_filter):
    offsets = jnp.arange(KL)[:, None] - jnp.arange(KL)[None, :]
    table = long_filter.astype(jnp.float32).T
    current = jnp.where(offsets >= 0, table[:, jnp.clip(offsets, 0, KL - 1)], 0.0)
    previous = jnp.where(offsets < 0, table[:, jnp.clip(offsets + KL, 0, KL - 1)], 0.0)
    return (current, previous)

def reference(tokens, norm_gain, w_in, short_filter, long_filter, w_out):
    wide_float = tokens.astype(jnp.float32)
    scale = lax.rsqrt(lax.optimization_barrier(jnp.mean(wide_float * wide_float, axis=-1, keepdims=True)) + 1e-06)
    normed = (wide_float * scale * norm_gain).astype(jnp.bfloat16)
    projected = jnp.dot(normed, w_in.reshape(D, 3 * D), preferred_element_type=jnp.float32)
    projected = projected.astype(jnp.bfloat16).reshape(TOKENS, 3, D)
    padded = jnp.pad(projected.astype(jnp.float32), ((KS - 1, 0), (0, 0), (0, 0)))
    featured = jnp.zeros((TOKENS, 3, D), jnp.float32)
    for tap in range(KS):
        featured = featured + short_filter[tap].astype(jnp.float32) * padded[KS - 1 - tap:KS - 1 - tap + TOKENS]
    mixed = (featured[:, 1] * featured[:, 2]).astype(jnp.bfloat16)
    current, previous = toeplitz_pair(long_filter)
    blocks = TOKENS // KL
    mixed_blocks = mixed.astype(jnp.float32).reshape(blocks, KL, G, GS)
    earlier = jnp.concatenate([jnp.zeros((1, KL, G, GS), jnp.float32), mixed_blocks[:-1]], axis=0)
    filtered = jnp.einsum('gts,bsgc->btgc', current, mixed_blocks)
    filtered = filtered + jnp.einsum('gts,bsgc->btgc', previous, earlier)
    gated = (featured[:, 0] * filtered.reshape(TOKENS, D)).astype(jnp.bfloat16)
    width_tp = D // N_TP
    summed = jnp.zeros((TOKENS, D), jnp.float32)
    for part in range(N_TP):
        term = jnp.dot(gated[:, part * width_tp:(part + 1) * width_tp], w_out[part * width_tp:(part + 1) * width_tp], preferred_element_type=jnp.float32)
        term = lax.optimization_barrier(term.astype(jnp.bfloat16))
        summed = summed + term.astype(jnp.float32)
    return (wide_float + summed).astype(jnp.bfloat16)
```

```python
import jax
import jax.numpy as jnp
from jax import lax
from jax.sharding import Mesh
from jax.sharding import PartitionSpec as P


def shifted(value, axis, steps):
    count = lax.axis_size(axis)
    first, last = (max(0, -steps), min(count, count - steps))
    return lax.ppermute(value, axis, [(source, source + steps) for source in range(first, last)])


def swap_pair(value):
    return lax.ppermute(value, "lo", [(0, 1), (1, 0)])


def toeplitz_pair(long_filter):
    filter_len, groups = long_filter.shape
    table = long_filter.T
    zeros = jnp.zeros((groups, filter_len), long_filter.dtype)

    def skew(edge):
        reverse = edge[:, ::-1]
        tiled = jnp.tile(reverse, (1, filter_len + 1))
        flat = tiled[:, filter_len - 1 : filter_len - 1 + filter_len * (2 * filter_len - 1)]
        return flat.reshape(groups, filter_len, 2 * filter_len - 1)[:, :, :filter_len]

    current = skew(jnp.concatenate([zeros, table], axis=1))
    previous = skew(jnp.concatenate([table, zeros], axis=1))
    return (current, previous)


def featurize(extended, short_filter, count):
    short_taps = short_filter.shape[0]
    ext_float = extended.astype(jnp.float32)
    featured = jnp.zeros((count,) + extended.shape[1:], jnp.float32)
    for tap in range(short_taps):
        featured = (
            featured
            + short_filter[tap] * ext_float[short_taps - 1 - tap : short_taps - 1 - tap + count]
        )
    return featured


def half_of(value, axis, half):
    size = value.shape[axis] // 2
    return lax.dynamic_slice_in_dim(value, half * size, size, axis)


def pair_ordered(mine, theirs, half, axis):
    first = jnp.where(half == 0, mine, theirs)
    second = jnp.where(half == 0, theirs, mine)
    return jnp.concatenate([first, second], axis=axis)


def local(tokens, norm_gain, w_in, short_filter, long_filter, w_out):
    own_rows, local_width = tokens.shape
    n_tp = lax.axis_size("tp")
    model_width = local_width * n_tp
    short_taps = short_filter.shape[0]
    filter_len = long_filter.shape[0]
    half = lax.axis_index("lo")
    other = 1 - half
    half_width = local_width // 2

    w_keep = half_of(w_in, 2, half)
    w_recv = swap_pair(half_of(w_in, 2, other))
    w_pair = pair_ordered(w_keep, w_recv, half, 0)
    w_full = lax.all_gather(w_pair, "hi", axis=0, tiled=True)

    o_keep = half_of(w_out, 0, half)
    o_recv = swap_pair(half_of(w_out, 0, other))
    o_pair = pair_ordered(o_keep, o_recv, half, 1)
    o_full = lax.all_gather(o_pair, "hi", axis=1, tiled=True)

    gathered = lax.all_gather(tokens, "tp", axis=1, tiled=True)
    pair_tokens = lax.all_gather(gathered, "lo", axis=0, tiled=True)
    row_count = pair_tokens.shape[0]
    wide_float = pair_tokens.astype(jnp.float32)
    scale = lax.rsqrt(jnp.mean(wide_float * wide_float, axis=-1, keepdims=True) + 1e-06)
    normed = (wide_float * scale * norm_gain).astype(jnp.bfloat16)

    projected = jnp.dot(
        normed, w_full.reshape(model_width, 3 * half_width), preferred_element_type=jnp.float32
    )
    projected = projected.astype(jnp.bfloat16).reshape(row_count, 3, half_width)

    taps = half_of(short_filter, 2, half)
    prior_rows = shifted(projected[row_count - (short_taps - 1) :], "hi", 1)
    featured = featurize(jnp.concatenate([prior_rows, projected], axis=0), taps, row_count)
    mixed = (featured[:, 1] * featured[:, 2]).astype(jnp.bfloat16)
    mixed_prior = shifted(mixed[row_count - (filter_len - 1) :], "hi", 1)
    query = featured[:, 0]
    zero_row = jnp.zeros((1, half_width), jnp.bfloat16)
    extended_mix = jnp.concatenate([zero_row, mixed_prior, mixed], axis=0)
    groups_here = long_filter.shape[1] // 2
    group_size = half_width // groups_here
    mix_blocks = extended_mix.reshape(
        row_count // filter_len + 1, filter_len, groups_here, group_size
    )
    current, previous = toeplitz_pair(half_of(long_filter, 1, half))
    filtered = jnp.einsum(
        "gts,bsgc->btgc", current, mix_blocks[1:], preferred_element_type=jnp.float32
    )
    filtered = filtered + jnp.einsum(
        "gts,bsgc->btgc", previous, mix_blocks[:-1], preferred_element_type=jnp.float32
    )
    gated = (query * filtered.reshape(row_count, half_width)).astype(jnp.bfloat16)

    terms = jnp.dot(gated, o_full, preferred_element_type=jnp.float32).astype(jnp.bfloat16)
    terms = terms.reshape(2, own_rows, n_tp, local_width).transpose(0, 2, 1, 3)
    terms = terms.reshape(2 * n_tp, own_rows, local_width)
    summed = lax.psum_scatter(terms, ("lo", "tp"), scatter_dimension=0, tiled=True)
    summed = summed.reshape(own_rows, local_width).astype(jnp.float32)
    return (tokens.astype(jnp.float32) + summed).astype(jnp.bfloat16)


def solution(mesh):
    n_ctx, n_tp = mesh.devices.shape
    paired = Mesh(mesh.devices.reshape(n_ctx // 2, 2, n_tp), ("hi", "lo", "tp"))
    ctx = ("hi", "lo")
    placed = (
        P(ctx, "tp"),
        P(),
        P(ctx, None, "tp"),
        P(None, None, "tp"),
        P(None, "tp"),
        P("tp", ctx),
    )
    return jax.shard_map(
        local, mesh=paired, in_specs=placed, out_specs=P(ctx, "tp"), check_vma=False
    )
```

```python
import jax
import jax.numpy as jnp
from jax import lax
from jax.sharding import Mesh
from jax.sharding import PartitionSpec as P


def shifted(value, axis, steps):
    count = lax.axis_size(axis)
    first, last = (max(0, -steps), min(count, count - steps))
    return lax.ppermute(value, axis, [(source, source + steps) for source in range(first, last)])


def swap_pair(value):
    return lax.ppermute(value, "lo", [(0, 1), (1, 0)])


def toeplitz_pair(long_filter):
    filter_len, groups = long_filter.shape
    table = long_filter.T
    zeros = jnp.zeros((groups, filter_len), long_filter.dtype)

    def skew(edge):
        reverse = edge[:, ::-1]
        tiled = jnp.tile(reverse, (1, filter_len + 1))
        flat = tiled[:, filter_len - 1 : filter_len - 1 + filter_len * (2 * filter_len - 1)]
        return flat.reshape(groups, filter_len, 2 * filter_len - 1)[:, :, :filter_len]

    current = skew(jnp.concatenate([zeros, table], axis=1))
    previous = skew(jnp.concatenate([table, zeros], axis=1))
    return (current, previous)


def featurize(extended, short_filter, count):
    short_taps = short_filter.shape[0]
    ext_float = extended.astype(jnp.float32)
    featured = jnp.zeros((count,) + extended.shape[1:], jnp.float32)
    for tap in range(short_taps):
        featured = (
            featured
            + short_filter[tap] * ext_float[short_taps - 1 - tap : short_taps - 1 - tap + count]
        )
    return featured


def half_of(value, axis, half):
    size = value.shape[axis] // 2
    return lax.dynamic_slice_in_dim(value, half * size, size, axis)


def pair_ordered(mine, theirs, half, axis):
    first = jnp.where(half == 0, mine, theirs)
    second = jnp.where(half == 0, theirs, mine)
    return jnp.concatenate([first, second], axis=axis)


def ring_order(count):
    return list(range(0, count, 2)) + list(range(count - 1 - count % 2, 0, -2))


def local(tokens, norm_gain, w_in, short_filter, long_filter, w_out):
    own_rows, local_width = tokens.shape
    n_tp = lax.axis_size("tp")
    n_hi = lax.axis_size("hi")
    model_width = local_width * n_tp
    short_taps = short_filter.shape[0]
    filter_len = long_filter.shape[0]
    w_rows = w_in.shape[0]
    half = lax.axis_index("lo")
    other = 1 - half
    half_width = local_width // 2

    pair_tokens = pair_ordered(tokens, swap_pair(tokens), half, 0)
    pair_tokens = lax.all_gather(pair_tokens, "tp", axis=1, tiled=True)
    row_count = pair_tokens.shape[0]
    wide_float = pair_tokens.astype(jnp.float32)
    scale = lax.rsqrt(jnp.mean(wide_float * wide_float, axis=-1, keepdims=True) + 1e-06)
    normed = (wide_float * scale * norm_gain).astype(jnp.bfloat16)

    own_piece = half_of(w_in, 2, half).reshape(w_rows, 3 * half_width)
    partner_piece = swap_pair(half_of(w_in, 2, other)).reshape(w_rows, 3 * half_width)
    order = ring_order(n_hi)
    place = [0] * n_hi
    for index, member in enumerate(order):
        place[member] = index
    order_table = jnp.array(order, jnp.int32)
    here = jnp.array(place, jnp.int32)[lax.axis_index("hi")]
    forward = [(order[i], order[(i + 1) % n_hi]) for i in range(n_hi)]
    backward = [(order[(i + 1) % n_hi], order[i]) for i in range(n_hi)]

    def contribution(piece, ctx_index):
        columns = lax.dynamic_slice_in_dim(normed, ctx_index * w_rows, w_rows, axis=1)
        return jnp.dot(columns, piece, preferred_element_type=jnp.float32)

    def ring_step(step, carry):
        own, partner, total = carry
        own_from = order_table[(here - step) % n_hi]
        partner_from = order_table[(here + step) % n_hi]
        total = total + contribution(own, 2 * own_from + half)
        total = total + contribution(partner, 2 * partner_from + other)
        own = lax.ppermute(own, "hi", forward)
        partner = lax.ppermute(partner, "hi", backward)
        return own, partner, total

    total = jnp.zeros((row_count, 3 * half_width), jnp.float32)
    own_piece, partner_piece, total = lax.fori_loop(
        0, n_hi - 1, ring_step, (own_piece, partner_piece, total)
    )
    last = n_hi - 1
    total = total + contribution(own_piece, 2 * order_table[(here - last) % n_hi] + half)
    projected = total + contribution(
        partner_piece, 2 * order_table[(here + last) % n_hi] + other
    )
    projected = projected.astype(jnp.bfloat16).reshape(row_count, 3, half_width)

    o_keep = half_of(w_out, 0, half)
    o_recv = swap_pair(half_of(w_out, 0, other))
    o_pair = pair_ordered(o_keep, o_recv, half, 1)
    o_full = lax.all_gather(o_pair, "hi", axis=1, tiled=True)

    taps = half_of(short_filter, 2, half)
    prior_rows = shifted(projected[row_count - (short_taps - 1) :], "hi", 1)
    featured = featurize(jnp.concatenate([prior_rows, projected], axis=0), taps, row_count)
    mixed = (featured[:, 1] * featured[:, 2]).astype(jnp.bfloat16)
    mixed_prior = shifted(mixed[row_count - (filter_len - 1) :], "hi", 1)
    query = featured[:, 0]
    zero_row = jnp.zeros((1, half_width), jnp.bfloat16)
    extended_mix = jnp.concatenate([zero_row, mixed_prior, mixed], axis=0)
    groups_here = long_filter.shape[1] // 2
    group_size = half_width // groups_here
    mix_blocks = extended_mix.reshape(
        row_count // filter_len + 1, filter_len, groups_here, group_size
    )
    current, previous = toeplitz_pair(half_of(long_filter, 1, half))
    filtered = jnp.einsum(
        "gts,bsgc->btgc", current, mix_blocks[1:], preferred_element_type=jnp.float32
    )
    filtered = filtered + jnp.einsum(
        "gts,bsgc->btgc", previous, mix_blocks[:-1], preferred_element_type=jnp.float32
    )
    gated = (query * filtered.reshape(row_count, half_width)).astype(jnp.bfloat16)

    terms = jnp.dot(gated, o_full, preferred_element_type=jnp.float32).astype(jnp.bfloat16)
    summed = lax.psum_scatter(terms, "tp", scatter_dimension=1, tiled=True)
    summed = lax.psum_scatter(summed, "lo", scatter_dimension=0, tiled=True)
    return (tokens.astype(jnp.float32) + summed.astype(jnp.float32)).astype(jnp.bfloat16)


def solution(mesh):
    n_ctx, n_tp = mesh.devices.shape
    paired = Mesh(mesh.devices.reshape(n_ctx // 2, 2, n_tp), ("hi", "lo", "tp"))
    ctx = ("hi", "lo")
    placed = (
        P(ctx, "tp"),
        P(),
        P(ctx, None, "tp"),
        P(None, None, "tp"),
        P(None, "tp"),
        P("tp", ctx),
    )
    return jax.shard_map(
        local, mesh=paired, in_specs=placed, out_specs=P(ctx, "tp"), check_vma=False
    )
```

```python
import jax
import jax.numpy as jnp
from jax import lax
from jax.sharding import Mesh
from jax.sharding import PartitionSpec as P


def shifted(value, axis, steps):
    count = lax.axis_size(axis)
    first, last = (max(0, -steps), min(count, count - steps))
    return lax.ppermute(value, axis, [(source, source + steps) for source in range(first, last)])


def swap_pair(value):
    return lax.ppermute(value, "lo", [(0, 1), (1, 0)])


def toeplitz_pair(long_filter):
    filter_len, groups = long_filter.shape
    table = long_filter.T
    zeros = jnp.zeros((groups, filter_len), long_filter.dtype)

    def skew(edge):
        reverse = edge[:, ::-1]
        tiled = jnp.tile(reverse, (1, filter_len + 1))
        flat = tiled[:, filter_len - 1 : filter_len - 1 + filter_len * (2 * filter_len - 1)]
        return flat.reshape(groups, filter_len, 2 * filter_len - 1)[:, :, :filter_len]

    current = skew(jnp.concatenate([zeros, table], axis=1))
    previous = skew(jnp.concatenate([table, zeros], axis=1))
    return (current, previous)


def featurize(extended, short_filter, count):
    short_taps = short_filter.shape[0]
    ext_float = extended.astype(jnp.float32)
    featured = jnp.zeros((count,) + extended.shape[1:], jnp.float32)
    for tap in range(short_taps):
        featured = (
            featured
            + short_filter[tap] * ext_float[short_taps - 1 - tap : short_taps - 1 - tap + count]
        )
    return featured


def half_of(value, axis, half):
    size = value.shape[axis] // 2
    return lax.dynamic_slice_in_dim(value, half * size, size, axis)


def pair_ordered(mine, theirs, half, axis):
    first = jnp.where(half == 0, mine, theirs)
    second = jnp.where(half == 0, theirs, mine)
    return jnp.concatenate([first, second], axis=axis)


def ring_order(count):
    return list(range(0, count, 2)) + list(range(count - 1 - count % 2, 0, -2))


def local(tokens, norm_gain, w_in, short_filter, long_filter, w_out):
    own_rows, local_width = tokens.shape
    n_tp = lax.axis_size("tp")
    n_hi = lax.axis_size("hi")
    model_width = local_width * n_tp
    short_taps = short_filter.shape[0]
    filter_len = long_filter.shape[0]
    w_rows = w_in.shape[0]
    half = lax.axis_index("lo")
    other = 1 - half
    half_width = local_width // 2

    pair_tokens = pair_ordered(tokens, swap_pair(tokens), half, 0)
    pair_tokens = lax.all_gather(pair_tokens, "tp", axis=1, tiled=True)
    row_count = pair_tokens.shape[0]
    wide_float = pair_tokens.astype(jnp.float32)
    scale = lax.rsqrt(jnp.mean(wide_float * wide_float, axis=-1, keepdims=True) + 1e-06)
    normed = (wide_float * scale * norm_gain).astype(jnp.bfloat16)

    own_piece = half_of(w_in, 2, half).reshape(w_rows, 3 * half_width)
    partner_piece = swap_pair(half_of(w_in, 2, other)).reshape(w_rows, 3 * half_width)
    order = ring_order(n_hi)
    place = [0] * n_hi
    for index, member in enumerate(order):
        place[member] = index
    order_table = jnp.array(order, jnp.int32)
    here = jnp.array(place, jnp.int32)[lax.axis_index("hi")]
    forward = [(order[i], order[(i + 1) % n_hi]) for i in range(n_hi)]
    backward = [(order[(i + 1) % n_hi], order[i]) for i in range(n_hi)]

    n_ctx = 2 * n_hi
    gathered_w = jnp.zeros((n_ctx, w_rows, 3 * half_width), jnp.bfloat16)

    def store(buffer, piece, ctx_index):
        return lax.dynamic_update_slice_in_dim(buffer, piece[None], ctx_index, axis=0)

    for step in range(n_hi):
        if step > 0:
            own_piece = lax.ppermute(own_piece, "hi", forward)
            partner_piece = lax.ppermute(partner_piece, "hi", backward)
        own_from = order_table[(here - step) % n_hi]
        partner_from = order_table[(here + step) % n_hi]
        gathered_w = store(gathered_w, own_piece, 2 * own_from + half)
        gathered_w = store(gathered_w, partner_piece, 2 * partner_from + other)
    projected = jnp.dot(
        normed,
        gathered_w.reshape(n_ctx * w_rows, 3 * half_width),
        preferred_element_type=jnp.float32,
    )
    projected = projected.astype(jnp.bfloat16).reshape(row_count, 3, half_width)

    o_keep = half_of(w_out, 0, half)
    o_recv = swap_pair(half_of(w_out, 0, other))
    o_pair = pair_ordered(o_keep, o_recv, half, 1)
    o_full = lax.all_gather(o_pair, "hi", axis=1, tiled=True)

    taps = half_of(short_filter, 2, half)
    prior_rows = shifted(projected[row_count - (short_taps - 1) :], "hi", 1)
    featured = featurize(jnp.concatenate([prior_rows, projected], axis=0), taps, row_count)
    mixed = (featured[:, 1] * featured[:, 2]).astype(jnp.bfloat16)
    mixed_prior = shifted(mixed[row_count - (filter_len - 1) :], "hi", 1)
    query = featured[:, 0]
    zero_row = jnp.zeros((1, half_width), jnp.bfloat16)
    extended_mix = jnp.concatenate([zero_row, mixed_prior, mixed], axis=0)
    groups_here = long_filter.shape[1] // 2
    group_size = half_width // groups_here
    mix_blocks = extended_mix.reshape(
        row_count // filter_len + 1, filter_len, groups_here, group_size
    )
    current, previous = toeplitz_pair(half_of(long_filter, 1, half))
    filtered = jnp.einsum(
        "gts,bsgc->btgc", current, mix_blocks[1:], preferred_element_type=jnp.float32
    )
    filtered = filtered + jnp.einsum(
        "gts,bsgc->btgc", previous, mix_blocks[:-1], preferred_element_type=jnp.float32
    )
    gated = (query * filtered.reshape(row_count, half_width)).astype(jnp.bfloat16)

    terms = jnp.dot(gated, o_full, preferred_element_type=jnp.float32).astype(jnp.bfloat16)
    summed = lax.psum_scatter(terms, "tp", scatter_dimension=1, tiled=True)
    summed = lax.psum_scatter(summed, "lo", scatter_dimension=0, tiled=True)
    return (tokens.astype(jnp.float32) + summed.astype(jnp.float32)).astype(jnp.bfloat16)


def solution(mesh):
    n_ctx, n_tp = mesh.devices.shape
    paired = Mesh(mesh.devices.reshape(n_ctx // 2, 2, n_tp), ("hi", "lo", "tp"))
    ctx = ("hi", "lo")
    placed = (
        P(ctx, "tp"),
        P(),
        P(ctx, None, "tp"),
        P(None, None, "tp"),
        P(None, "tp"),
        P("tp", ctx),
    )
    return jax.shard_map(
        local, mesh=paired, in_specs=placed, out_specs=P(ctx, "tp"), check_vma=False
    )
```

```python
import jax
import jax.numpy as jnp
from jax import lax
from jax.sharding import Mesh
from jax.sharding import PartitionSpec as P


def shifted(value, axis, steps):
    count = lax.axis_size(axis)
    first, last = (max(0, -steps), min(count, count - steps))
    return lax.ppermute(value, axis, [(source, source + steps) for source in range(first, last)])


def swap_pair(value):
    return lax.ppermute(value, "lo", [(0, 1), (1, 0)])


def toeplitz_pair(long_filter):
    filter_len, groups = long_filter.shape
    table = long_filter.T
    zeros = jnp.zeros((groups, filter_len), long_filter.dtype)

    def skew(edge):
        reverse = edge[:, ::-1]
        tiled = jnp.tile(reverse, (1, filter_len + 1))
        flat = tiled[:, filter_len - 1 : filter_len - 1 + filter_len * (2 * filter_len - 1)]
        return flat.reshape(groups, filter_len, 2 * filter_len - 1)[:, :, :filter_len]

    current = skew(jnp.concatenate([zeros, table], axis=1))
    previous = skew(jnp.concatenate([table, zeros], axis=1))
    return (current, previous)


def featurize(extended, short_filter, count):
    short_taps = short_filter.shape[0]
    ext_float = extended.astype(jnp.float32)
    featured = jnp.zeros((count,) + extended.shape[1:], jnp.float32)
    for tap in range(short_taps):
        featured = (
            featured
            + short_filter[tap] * ext_float[short_taps - 1 - tap : short_taps - 1 - tap + count]
        )
    return featured


def half_of(value, axis, half):
    size = value.shape[axis] // 2
    return lax.dynamic_slice_in_dim(value, half * size, size, axis)


def pair_ordered(mine, theirs, half, axis):
    first = jnp.where(half == 0, mine, theirs)
    second = jnp.where(half == 0, theirs, mine)
    return jnp.concatenate([first, second], axis=axis)


def ring_order(count):
    return list(range(0, count, 2)) + list(range(count - 1 - count % 2, 0, -2))


def local(tokens, norm_gain, w_in, short_filter, long_filter, w_out):
    own_rows, local_width = tokens.shape
    n_tp = lax.axis_size("tp")
    n_hi = lax.axis_size("hi")
    model_width = local_width * n_tp
    short_taps = short_filter.shape[0]
    filter_len = long_filter.shape[0]
    w_rows = w_in.shape[0]
    half = lax.axis_index("lo")
    other = 1 - half
    half_width = local_width // 2

    pair_tokens = pair_ordered(tokens, swap_pair(tokens), half, 0)
    pair_tokens = lax.all_gather(pair_tokens, "tp", axis=1, tiled=True)
    row_count = pair_tokens.shape[0]
    wide_float = pair_tokens.astype(jnp.float32)
    scale = lax.rsqrt(jnp.mean(wide_float * wide_float, axis=-1, keepdims=True) + 1e-06)
    normed = (wide_float * scale * norm_gain).astype(jnp.bfloat16)

    own_piece = half_of(w_in, 2, half).reshape(w_rows, 3 * half_width)
    partner_piece = swap_pair(half_of(w_in, 2, other)).reshape(w_rows, 3 * half_width)
    order = ring_order(n_hi)
    place = [0] * n_hi
    for index, member in enumerate(order):
        place[member] = index
    order_table = jnp.array(order, jnp.int32)
    here = jnp.array(place, jnp.int32)[lax.axis_index("hi")]
    forward = [(order[i], order[(i + 1) % n_hi]) for i in range(n_hi)]
    backward = [(order[(i + 1) % n_hi], order[i]) for i in range(n_hi)]

    n_ctx = 2 * n_hi
    gathered_w = jnp.zeros((n_ctx, w_rows, 3 * half_width), jnp.bfloat16)

    def store(buffer, piece, ctx_index):
        return lax.dynamic_update_slice_in_dim(buffer, piece[None], ctx_index, axis=0)

    current, previous = toeplitz_pair(half_of(long_filter, 1, half))
    for step in range(n_hi):
        if step > 0:
            own_piece = lax.ppermute(own_piece, "hi", forward)
            partner_piece = lax.ppermute(partner_piece, "hi", backward)
        if step == 1:
            own_piece, partner_piece, current, previous = lax.optimization_barrier(
                (own_piece, partner_piece, current, previous)
            )
        own_from = order_table[(here - step) % n_hi]
        partner_from = order_table[(here + step) % n_hi]
        gathered_w = store(gathered_w, own_piece, 2 * own_from + half)
        gathered_w = store(gathered_w, partner_piece, 2 * partner_from + other)
    projected = jnp.dot(
        normed,
        gathered_w.reshape(n_ctx * w_rows, 3 * half_width),
        preferred_element_type=jnp.float32,
    )
    projected = projected.astype(jnp.bfloat16).reshape(row_count, 3, half_width)

    o_keep = half_of(w_out, 0, half)
    o_recv = swap_pair(half_of(w_out, 0, other))
    o_pair = pair_ordered(o_keep, o_recv, half, 1)
    o_full = lax.all_gather(o_pair, "hi", axis=1, tiled=True)

    taps = half_of(short_filter, 2, half)
    prior_rows = shifted(projected[row_count - (short_taps - 1) :], "hi", 1)
    featured = featurize(jnp.concatenate([prior_rows, projected], axis=0), taps, row_count)
    mixed = (featured[:, 1] * featured[:, 2]).astype(jnp.bfloat16)
    mixed_prior = shifted(mixed[row_count - (filter_len - 1) :], "hi", 1)
    query = featured[:, 0]
    zero_row = jnp.zeros((1, half_width), jnp.bfloat16)
    extended_mix = jnp.concatenate([zero_row, mixed_prior, mixed], axis=0)
    groups_here = long_filter.shape[1] // 2
    group_size = half_width // groups_here
    mix_blocks = extended_mix.reshape(
        row_count // filter_len + 1, filter_len, groups_here, group_size
    )
    filtered = jnp.einsum(
        "gts,bsgc->btgc", current, mix_blocks[1:], preferred_element_type=jnp.float32
    )
    filtered = filtered + jnp.einsum(
        "gts,bsgc->btgc", previous, mix_blocks[:-1], preferred_element_type=jnp.float32
    )
    gated = (query * filtered.reshape(row_count, half_width)).astype(jnp.bfloat16)

    def out_terms(rows):
        terms = jnp.dot(rows, o_full, preferred_element_type=jnp.float32).astype(jnp.bfloat16)
        return lax.psum_scatter(terms, "tp", scatter_dimension=1, tiled=True)

    arrived = swap_pair(out_terms(half_of(gated, 0, other)))
    summed = out_terms(half_of(gated, 0, half)).astype(jnp.float32) + arrived.astype(jnp.float32)
    return (tokens.astype(jnp.float32) + summed).astype(jnp.bfloat16)


def solution(mesh):
    n_ctx, n_tp = mesh.devices.shape
    paired = Mesh(mesh.devices.reshape(n_ctx // 2, 2, n_tp), ("hi", "lo", "tp"))
    ctx = ("hi", "lo")
    placed = (
        P(ctx, "tp"),
        P(),
        P(ctx, None, "tp"),
        P(None, None, "tp"),
        P(None, "tp"),
        P("tp", ctx),
    )
    return jax.shard_map(
        local, mesh=paired, in_specs=placed, out_specs=P(ctx, "tp"), check_vma=False
    )
```

```python
import jax
import jax.numpy as jnp
from jax import lax
from jax.sharding import Mesh
from jax.sharding import PartitionSpec as P


def shifted(value, axis, steps):
    count = lax.axis_size(axis)
    first, last = (max(0, -steps), min(count, count - steps))
    return lax.ppermute(value, axis, [(source, source + steps) for source in range(first, last)])


def swap_pair(value):
    return lax.ppermute(value, "lo", [(0, 1), (1, 0)])


def toeplitz_pair(long_filter):
    filter_len, groups = long_filter.shape
    table = long_filter.T
    zeros = jnp.zeros((groups, filter_len), long_filter.dtype)

    def skew(edge):
        reverse = edge[:, ::-1]
        tiled = jnp.tile(reverse, (1, filter_len + 1))
        flat = tiled[:, filter_len - 1 : filter_len - 1 + filter_len * (2 * filter_len - 1)]
        return flat.reshape(groups, filter_len, 2 * filter_len - 1)[:, :, :filter_len]

    current = skew(jnp.concatenate([zeros, table], axis=1))
    previous = skew(jnp.concatenate([table, zeros], axis=1))
    return (current, previous)


def featurize(extended, short_filter, count):
    short_taps = short_filter.shape[0]
    ext_float = extended.astype(jnp.float32)
    featured = jnp.zeros((count,) + extended.shape[1:], jnp.float32)
    for tap in range(short_taps):
        featured = (
            featured
            + short_filter[tap] * ext_float[short_taps - 1 - tap : short_taps - 1 - tap + count]
        )
    return featured


def half_of(value, axis, half):
    size = value.shape[axis] // 2
    return lax.dynamic_slice_in_dim(value, half * size, size, axis)


def pair_ordered(mine, theirs, half, axis):
    first = jnp.where(half == 0, mine, theirs)
    second = jnp.where(half == 0, theirs, mine)
    return jnp.concatenate([first, second], axis=axis)


def ring_order(count):
    return list(range(0, count, 2)) + list(range(count - 1 - count % 2, 0, -2))


def local(tokens, norm_gain, w_in, short_filter, long_filter, w_out):
    own_rows, local_width = tokens.shape
    n_tp = lax.axis_size("tp")
    n_hi = lax.axis_size("hi")
    model_width = local_width * n_tp
    short_taps = short_filter.shape[0]
    filter_len = long_filter.shape[0]
    w_rows = w_in.shape[0]
    half = lax.axis_index("lo")
    other = 1 - half
    half_width = local_width // 2

    own_piece = half_of(w_in, 2, half).reshape(w_rows, 3 * half_width)
    partner_piece = swap_pair(half_of(w_in, 2, other)).reshape(w_rows, 3 * half_width)
    order = ring_order(n_hi)
    place = [0] * n_hi
    for index, member in enumerate(order):
        place[member] = index
    order_table = jnp.array(order, jnp.int32)
    here = jnp.array(place, jnp.int32)[lax.axis_index("hi")]
    forward = [(order[i], order[(i + 1) % n_hi]) for i in range(n_hi)]
    backward = [(order[(i + 1) % n_hi], order[i]) for i in range(n_hi)]

    n_ctx = 2 * n_hi
    gathered_w = jnp.zeros((n_ctx, w_rows, 3 * half_width), jnp.bfloat16)

    def store(buffer, piece, ctx_index):
        return lax.dynamic_update_slice_in_dim(buffer, piece[None], ctx_index, axis=0)

    current, previous = toeplitz_pair(half_of(long_filter, 1, half))
    for step in range(n_hi):
        if step > 0:
            own_piece = lax.ppermute(own_piece, "hi", forward)
            partner_piece = lax.ppermute(partner_piece, "hi", backward)
        own_stored, partner_stored = own_piece, partner_piece
        if step == 1:
            own_stored, partner_stored, current, previous, tokens_late = lax.optimization_barrier(
                (own_piece, partner_piece, current, previous, tokens)
            )
        if step == n_hi - 1:
            w_out_late, own_stored = lax.optimization_barrier((w_out, own_piece))
        own_from = order_table[(here - step) % n_hi]
        partner_from = order_table[(here + step) % n_hi]
        gathered_w = store(gathered_w, own_stored, 2 * own_from + half)
        gathered_w = store(gathered_w, partner_stored, 2 * partner_from + other)

    pair_tokens = pair_ordered(tokens_late, swap_pair(tokens_late), half, 0)
    pair_tokens = lax.all_gather(pair_tokens, "tp", axis=1, tiled=True)
    row_count = pair_tokens.shape[0]
    wide_float = pair_tokens.astype(jnp.float32)
    scale = lax.rsqrt(jnp.mean(wide_float * wide_float, axis=-1, keepdims=True) + 1e-06)
    normed = (wide_float * scale * norm_gain).astype(jnp.bfloat16)

    o_keep = half_of(w_out_late, 0, half)
    o_recv = swap_pair(half_of(w_out_late, 0, other))
    o_pair = pair_ordered(o_keep, o_recv, half, 1)
    o_full = lax.all_gather(o_pair, "hi", axis=1, tiled=True)

    projected = jnp.dot(
        normed,
        gathered_w.reshape(n_ctx * w_rows, 3 * half_width),
        preferred_element_type=jnp.float32,
    )
    projected = projected.astype(jnp.bfloat16).reshape(row_count, 3, half_width)

    taps = half_of(short_filter, 2, half)
    prior_rows = shifted(projected[row_count - (short_taps - 1) :], "hi", 1)
    featured = featurize(jnp.concatenate([prior_rows, projected], axis=0), taps, row_count)
    mixed = (featured[:, 1] * featured[:, 2]).astype(jnp.bfloat16)
    mixed_prior = shifted(mixed[row_count - (filter_len - 1) :], "hi", 1)
    query = featured[:, 0]
    zero_row = jnp.zeros((1, half_width), jnp.bfloat16)
    extended_mix = jnp.concatenate([zero_row, mixed_prior, mixed], axis=0)
    groups_here = long_filter.shape[1] // 2
    group_size = half_width // groups_here
    mix_blocks = extended_mix.reshape(
        row_count // filter_len + 1, filter_len, groups_here, group_size
    )
    filtered = jnp.einsum(
        "gts,bsgc->btgc", current, mix_blocks[1:], preferred_element_type=jnp.float32
    )
    filtered = filtered + jnp.einsum(
        "gts,bsgc->btgc", previous, mix_blocks[:-1], preferred_element_type=jnp.float32
    )
    gated = (query * filtered.reshape(row_count, half_width)).astype(jnp.bfloat16)

    def out_terms(rows):
        terms = jnp.dot(rows, o_full, preferred_element_type=jnp.float32).astype(jnp.bfloat16)
        return lax.psum_scatter(terms, "tp", scatter_dimension=1, tiled=True)

    arrived = swap_pair(out_terms(half_of(gated, 0, other)))
    summed = out_terms(half_of(gated, 0, half)).astype(jnp.float32) + arrived.astype(jnp.float32)
    return (tokens.astype(jnp.float32) + summed).astype(jnp.bfloat16)


def solution(mesh):
    n_ctx, n_tp = mesh.devices.shape
    paired = Mesh(mesh.devices.reshape(n_ctx // 2, 2, n_tp), ("hi", "lo", "tp"))
    ctx = ("hi", "lo")
    placed = (
        P(ctx, "tp"),
        P(),
        P(ctx, None, "tp"),
        P(None, None, "tp"),
        P(None, "tp"),
        P("tp", ctx),
    )
    return jax.shard_map(
        local, mesh=paired, in_specs=placed, out_specs=P(ctx, "tp"), check_vma=False
    )
```

```python
import jax
import jax.numpy as jnp
from jax import lax
from jax.sharding import Mesh
from jax.sharding import PartitionSpec as P


def shifted(value, axis, steps):
    count = lax.axis_size(axis)
    first, last = (max(0, -steps), min(count, count - steps))
    return lax.ppermute(value, axis, [(source, source + steps) for source in range(first, last)])


def swap_pair(value):
    return lax.ppermute(value, "lo", [(0, 1), (1, 0)])


def toeplitz_pair(long_filter):
    filter_len = long_filter.shape[0]
    tap = lax.broadcasted_iota(jnp.int32, (filter_len, filter_len, filter_len), 0)
    offset = lax.broadcasted_iota(jnp.int32, (filter_len, filter_len, filter_len), 1) - (
        lax.broadcasted_iota(jnp.int32, (filter_len, filter_len, filter_len), 2)
    )
    table = long_filter.T

    def spread(hot):
        dense = jnp.einsum(
            "gm,mts->gts", table, hot.astype(table.dtype), preferred_element_type=jnp.float32
        )
        return dense.astype(table.dtype)

    return (spread(offset == tap), spread(offset + filter_len == tap))


def featurize(extended, short_filter, count):
    short_taps = short_filter.shape[0]
    ext_float = extended.astype(jnp.float32)
    featured = jnp.zeros((count,) + extended.shape[1:], jnp.float32)
    for tap in range(short_taps):
        featured = (
            featured
            + short_filter[tap] * ext_float[short_taps - 1 - tap : short_taps - 1 - tap + count]
        )
    return featured


def half_of(value, axis, half):
    size = value.shape[axis] // 2
    return lax.dynamic_slice_in_dim(value, half * size, size, axis)


def pair_ordered(mine, theirs, half, axis):
    first = jnp.where(half == 0, mine, theirs)
    second = jnp.where(half == 0, theirs, mine)
    return jnp.concatenate([first, second], axis=axis)


def ring_order(count):
    return list(range(0, count, 2)) + list(range(count - 1 - count % 2, 0, -2))


def local(tokens, norm_gain, w_in, short_filter, long_filter, w_out):
    own_rows, local_width = tokens.shape
    n_tp = lax.axis_size("tp")
    n_hi = lax.axis_size("hi")
    model_width = local_width * n_tp
    short_taps = short_filter.shape[0]
    filter_len = long_filter.shape[0]
    w_rows = w_in.shape[0]
    half = lax.axis_index("lo")
    other = 1 - half
    half_width = local_width // 2

    pair_tokens = pair_ordered(tokens, swap_pair(tokens), half, 0)
    pair_tokens = lax.all_gather(pair_tokens, "tp", axis=1, tiled=True)
    row_count = pair_tokens.shape[0]
    wide_float = pair_tokens.astype(jnp.float32)
    scale = lax.rsqrt(jnp.mean(wide_float * wide_float, axis=-1, keepdims=True) + 1e-06)
    normed = (wide_float * scale * norm_gain).astype(jnp.bfloat16)

    own_piece = half_of(w_in, 2, half).reshape(w_rows, 3 * half_width)
    partner_piece = swap_pair(half_of(w_in, 2, other)).reshape(w_rows, 3 * half_width)
    order = ring_order(n_hi)
    place = [0] * n_hi
    for index, member in enumerate(order):
        place[member] = index
    order_table = jnp.array(order, jnp.int32)
    here = jnp.array(place, jnp.int32)[lax.axis_index("hi")]
    forward = [(order[i], order[(i + 1) % n_hi]) for i in range(n_hi)]
    backward = [(order[(i + 1) % n_hi], order[i]) for i in range(n_hi)]

    n_ctx = 2 * n_hi
    gathered_w = jnp.zeros((n_ctx, w_rows, 3 * half_width), jnp.bfloat16)

    def store(buffer, piece, ctx_index):
        return lax.dynamic_update_slice_in_dim(buffer, piece[None], ctx_index, axis=0)

    current, previous = toeplitz_pair(half_of(long_filter, 1, half))
    for step in range(n_hi):
        if step > 0:
            own_piece = lax.ppermute(own_piece, "hi", forward)
            partner_piece = lax.ppermute(partner_piece, "hi", backward)
        own_from = order_table[(here - step) % n_hi]
        partner_from = order_table[(here + step) % n_hi]
        gathered_w = store(gathered_w, own_piece, 2 * own_from + half)
        gathered_w = store(gathered_w, partner_piece, 2 * partner_from + other)
    projected = jnp.dot(
        normed,
        gathered_w.reshape(n_ctx * w_rows, 3 * half_width),
        preferred_element_type=jnp.float32,
    )
    projected = projected.astype(jnp.bfloat16).reshape(row_count, 3, half_width)

    o_keep = half_of(w_out, 0, half)
    o_recv = swap_pair(half_of(w_out, 0, other))
    o_pair = pair_ordered(o_keep, o_recv, half, 1)
    o_full = lax.all_gather(o_pair, "hi", axis=1, tiled=True)

    taps = half_of(short_filter, 2, half)
    prior_rows = shifted(projected[row_count - (short_taps - 1) :], "hi", 1)
    featured = featurize(jnp.concatenate([prior_rows, projected], axis=0), taps, row_count)
    mixed = (featured[:, 1] * featured[:, 2]).astype(jnp.bfloat16)
    mixed_prior = shifted(mixed[row_count - (filter_len - 1) :], "hi", 1)
    query = featured[:, 0]
    zero_row = jnp.zeros((1, half_width), jnp.bfloat16)
    extended_mix = jnp.concatenate([zero_row, mixed_prior, mixed], axis=0)
    groups_here = long_filter.shape[1] // 2
    group_size = half_width // groups_here
    mix_blocks = extended_mix.reshape(
        row_count // filter_len + 1, filter_len, groups_here, group_size
    )
    filtered = jnp.einsum(
        "gts,bsgc->btgc", current, mix_blocks[1:], preferred_element_type=jnp.float32
    )
    filtered = filtered + jnp.einsum(
        "gts,bsgc->btgc", previous, mix_blocks[:-1], preferred_element_type=jnp.float32
    )
    gated = (query * filtered.reshape(row_count, half_width)).astype(jnp.bfloat16)

    def out_terms(rows):
        terms = jnp.dot(rows, o_full, preferred_element_type=jnp.float32).astype(jnp.bfloat16)
        return lax.psum_scatter(terms, "tp", scatter_dimension=1, tiled=True)

    arrived = swap_pair(out_terms(half_of(gated, 0, other)))
    summed = out_terms(half_of(gated, 0, half)).astype(jnp.float32) + arrived.astype(jnp.float32)
    return (tokens.astype(jnp.float32) + summed).astype(jnp.bfloat16)


def solution(mesh):
    n_ctx, n_tp = mesh.devices.shape
    paired = Mesh(mesh.devices.reshape(n_ctx // 2, 2, n_tp), ("hi", "lo", "tp"))
    ctx = ("hi", "lo")
    placed = (
        P(ctx, "tp"),
        P(),
        P(ctx, None, "tp"),
        P(None, None, "tp"),
        P(None, "tp"),
        P("tp", ctx),
    )
    return jax.shard_map(
        local, mesh=paired, in_specs=placed, out_specs=P(ctx, "tp"), check_vma=False
    )
```

```python
import jax
import jax.numpy as jnp
from jax import lax
from jax.sharding import Mesh
from jax.sharding import PartitionSpec as P


def shifted(value, axis, steps):
    count = lax.axis_size(axis)
    first, last = (max(0, -steps), min(count, count - steps))
    return lax.ppermute(value, axis, [(source, source + steps) for source in range(first, last)])


def swap_pair(value):
    return lax.ppermute(value, "lo", [(0, 1), (1, 0)])


def toeplitz_pair(long_filter):
    filter_len = long_filter.shape[0]
    tap = lax.broadcasted_iota(jnp.int32, (filter_len, filter_len, filter_len), 0)
    offset = lax.broadcasted_iota(jnp.int32, (filter_len, filter_len, filter_len), 1) - (
        lax.broadcasted_iota(jnp.int32, (filter_len, filter_len, filter_len), 2)
    )
    table = long_filter.T

    def spread(hot):
        return jnp.einsum("gm,mts->gts", table, hot.astype(table.dtype))

    return (spread(offset == tap), spread(offset + filter_len == tap))


def featurize(extended, short_filter, count):
    short_taps = short_filter.shape[0]
    ext_float = extended.astype(jnp.float32)
    featured = jnp.zeros((count,) + extended.shape[1:], jnp.float32)
    for tap in range(short_taps):
        featured = (
            featured
            + short_filter[tap] * ext_float[short_taps - 1 - tap : short_taps - 1 - tap + count]
        )
    return featured


def half_of(value, axis, half):
    size = value.shape[axis] // 2
    return lax.dynamic_slice_in_dim(value, half * size, size, axis)


def pair_ordered(mine, theirs, half, axis):
    first = jnp.where(half == 0, mine, theirs)
    second = jnp.where(half == 0, theirs, mine)
    return jnp.concatenate([first, second], axis=axis)


def ring_order(count):
    return list(range(0, count, 2)) + list(range(count - 1 - count % 2, 0, -2))


def local(tokens, norm_gain, w_in, short_filter, long_filter, w_out):
    own_rows, local_width = tokens.shape
    n_tp = lax.axis_size("tp")
    n_hi = lax.axis_size("hi")
    model_width = local_width * n_tp
    short_taps = short_filter.shape[0]
    filter_len = long_filter.shape[0]
    w_rows = w_in.shape[0]
    half = lax.axis_index("lo")
    other = 1 - half
    half_width = local_width // 2

    pair_tokens = lax.all_gather(tokens, "lo", axis=0, tiled=True)
    pair_tokens = lax.all_gather(pair_tokens, "tp", axis=1, tiled=True)
    row_count = pair_tokens.shape[0]
    wide_float = pair_tokens.astype(jnp.float32)
    scale = lax.rsqrt(jnp.mean(wide_float * wide_float, axis=-1, keepdims=True) + 1e-06)
    normed = (wide_float * scale * norm_gain).astype(jnp.bfloat16)

    own_piece = half_of(w_in, 2, half).reshape(w_rows, 3 * half_width)
    partner_piece = swap_pair(half_of(w_in, 2, other)).reshape(w_rows, 3 * half_width)
    order = ring_order(n_hi)
    place = [0] * n_hi
    for index, member in enumerate(order):
        place[member] = index
    order_table = jnp.array(order, jnp.int32)
    here = jnp.array(place, jnp.int32)[lax.axis_index("hi")]
    forward = [(order[i], order[(i + 1) % n_hi]) for i in range(n_hi)]
    backward = [(order[(i + 1) % n_hi], order[i]) for i in range(n_hi)]

    e_cols = w_out.shape[1]
    own_out = half_of(w_out, 0, half)
    partner_out = swap_pair(half_of(w_out, 0, other))

    n_ctx = 2 * n_hi
    gathered_w = jnp.zeros((n_ctx, w_rows, 3 * half_width), jnp.bfloat16)
    gathered_o = jnp.zeros((half_width, n_ctx, e_cols), jnp.bfloat16)

    def store(buffer, piece, ctx_index):
        return lax.dynamic_update_slice_in_dim(buffer, piece[None], ctx_index, axis=0)

    def store_out(buffer, piece, ctx_index):
        return lax.dynamic_update_slice_in_dim(buffer, piece[:, None], ctx_index, axis=1)

    current, previous = toeplitz_pair(half_of(long_filter, 1, half))
    for step in range(n_hi):
        if step > 0:
            own_piece = lax.ppermute(own_piece, "hi", forward)
            partner_piece = lax.ppermute(partner_piece, "hi", backward)
            own_out = lax.ppermute(own_out, "hi", forward)
            partner_out = lax.ppermute(partner_out, "hi", backward)
        own_at = 2 * order_table[(here - step) % n_hi] + half
        partner_at = 2 * order_table[(here + step) % n_hi] + other
        gathered_w = store(gathered_w, own_piece, own_at)
        gathered_w = store(gathered_w, partner_piece, partner_at)
        gathered_o = store_out(gathered_o, own_out, own_at)
        gathered_o = store_out(gathered_o, partner_out, partner_at)
    o_full = gathered_o.reshape(half_width, n_ctx * e_cols)

    projected = jnp.dot(
        normed,
        gathered_w.reshape(n_ctx * w_rows, 3 * half_width),
        preferred_element_type=jnp.float32,
    )
    projected = projected.astype(jnp.bfloat16).reshape(row_count, 3, half_width)

    taps = half_of(short_filter, 2, half)
    prior_rows = shifted(projected[row_count - (short_taps - 1) :], "hi", 1)
    featured = featurize(jnp.concatenate([prior_rows, projected], axis=0), taps, row_count)
    mixed = (featured[:, 1] * featured[:, 2]).astype(jnp.bfloat16)
    mixed_prior = shifted(mixed[row_count - (filter_len - 1) :], "hi", 1)
    query = featured[:, 0]
    zero_row = jnp.zeros((1, half_width), jnp.bfloat16)
    extended_mix = jnp.concatenate([zero_row, mixed_prior, mixed], axis=0)
    groups_here = long_filter.shape[1] // 2
    group_size = half_width // groups_here
    mix_blocks = extended_mix.reshape(
        row_count // filter_len + 1, filter_len, groups_here, group_size
    )
    filtered = jnp.einsum(
        "gts,bsgc->btgc", current, mix_blocks[1:], preferred_element_type=jnp.float32
    )
    filtered = filtered + jnp.einsum(
        "gts,bsgc->btgc", previous, mix_blocks[:-1], preferred_element_type=jnp.float32
    )
    gated = (query * filtered.reshape(row_count, half_width)).astype(jnp.bfloat16)

    def out_terms(rows):
        terms = jnp.dot(rows, o_full, preferred_element_type=jnp.float32).astype(jnp.bfloat16)
        return lax.psum_scatter(terms, "tp", scatter_dimension=1, tiled=True)

    arrived = swap_pair(out_terms(half_of(gated, 0, other)))
    summed = out_terms(half_of(gated, 0, half)).astype(jnp.float32) + arrived.astype(jnp.float32)
    return (tokens.astype(jnp.float32) + summed).astype(jnp.bfloat16)


def solution(mesh):
    n_ctx, n_tp = mesh.devices.shape
    paired = Mesh(mesh.devices.reshape(n_ctx // 2, 2, n_tp), ("hi", "lo", "tp"))
    ctx = ("hi", "lo")
    placed = (
        P(ctx, "tp"),
        P(),
        P(ctx, None, "tp"),
        P(None, None, "tp"),
        P(None, "tp"),
        P("tp", ctx),
    )
    return jax.shard_map(
        local, mesh=paired, in_specs=placed, out_specs=P(ctx, "tp"), check_vma=False
    )
```

```python
import jax
import jax.numpy as jnp
from jax import lax
from jax.sharding import Mesh
from jax.sharding import PartitionSpec as P


def shifted(value, axis, steps):
    count = lax.axis_size(axis)
    first, last = (max(0, -steps), min(count, count - steps))
    return lax.ppermute(value, axis, [(source, source + steps) for source in range(first, last)])


def swap_pair(value):
    return lax.ppermute(value, "lo", [(0, 1), (1, 0)])


def toeplitz_pair(long_filter):
    filter_len = long_filter.shape[0]
    tap = lax.broadcasted_iota(jnp.int32, (filter_len, filter_len, filter_len), 0)
    offset = lax.broadcasted_iota(jnp.int32, (filter_len, filter_len, filter_len), 1) - (
        lax.broadcasted_iota(jnp.int32, (filter_len, filter_len, filter_len), 2)
    )
    table = long_filter.T

    def spread(hot):
        return jnp.einsum("gm,mts->gts", table, hot.astype(table.dtype))

    return (spread(offset == tap), spread(offset + filter_len == tap))


def featurize(extended, short_filter, count):
    short_taps = short_filter.shape[0]
    ext_float = extended.astype(jnp.float32)
    featured = jnp.zeros((count,) + extended.shape[1:], jnp.float32)
    for tap in range(short_taps):
        featured = (
            featured
            + short_filter[tap] * ext_float[short_taps - 1 - tap : short_taps - 1 - tap + count]
        )
    return featured


def half_of(value, axis, half):
    size = value.shape[axis] // 2
    return lax.dynamic_slice_in_dim(value, half * size, size, axis)


def pair_ordered(mine, theirs, half, axis):
    first = jnp.where(half == 0, mine, theirs)
    second = jnp.where(half == 0, theirs, mine)
    return jnp.concatenate([first, second], axis=axis)


def ring_order(count):
    return list(range(0, count, 2)) + list(range(count - 1 - count % 2, 0, -2))


def local(tokens, norm_gain, w_in, short_filter, long_filter, w_out):
    own_rows, local_width = tokens.shape
    n_tp = lax.axis_size("tp")
    n_hi = lax.axis_size("hi")
    model_width = local_width * n_tp
    short_taps = short_filter.shape[0]
    filter_len = long_filter.shape[0]
    w_rows = w_in.shape[0]
    half = lax.axis_index("lo")
    other = 1 - half
    half_width = local_width // 2

    pair_tokens = lax.all_gather(tokens, ("lo", "tp"), axis=0, tiled=False)
    pair_tokens = pair_tokens.reshape(2, n_tp, own_rows, local_width).transpose(0, 2, 1, 3)
    row_count = 2 * own_rows
    pair_tokens = pair_tokens.reshape(row_count, model_width)
    wide_float = pair_tokens.astype(jnp.float32)
    scale = lax.rsqrt(jnp.mean(wide_float * wide_float, axis=-1, keepdims=True) + 1e-06)
    normed = (wide_float * scale * norm_gain).astype(jnp.bfloat16)

    own_piece = half_of(w_in, 2, half).reshape(w_rows, 3 * half_width)
    partner_piece = swap_pair(half_of(w_in, 2, other)).reshape(w_rows, 3 * half_width)
    order = ring_order(n_hi)
    place = [0] * n_hi
    for index, member in enumerate(order):
        place[member] = index
    order_table = jnp.array(order, jnp.int32)
    here = jnp.array(place, jnp.int32)[lax.axis_index("hi")]
    forward = [(order[i], order[(i + 1) % n_hi]) for i in range(n_hi)]
    backward = [(order[(i + 1) % n_hi], order[i]) for i in range(n_hi)]

    e_cols = w_out.shape[1]
    own_out = half_of(w_out, 0, half)
    partner_out = swap_pair(half_of(w_out, 0, other))

    n_ctx = 2 * n_hi
    gathered_w = jnp.zeros((n_ctx, w_rows, 3 * half_width), jnp.bfloat16)
    gathered_o = jnp.zeros((half_width, n_ctx, e_cols), jnp.bfloat16)

    def store(buffer, piece, ctx_index):
        return lax.dynamic_update_slice_in_dim(buffer, piece[None], ctx_index, axis=0)

    def store_out(buffer, piece, ctx_index):
        return lax.dynamic_update_slice_in_dim(buffer, piece[:, None], ctx_index, axis=1)

    current, previous = toeplitz_pair(half_of(long_filter, 1, half))
    for step in range(n_hi):
        if step > 0:
            own_piece = lax.ppermute(own_piece, "hi", forward)
            partner_piece = lax.ppermute(partner_piece, "hi", backward)
            own_out = lax.ppermute(own_out, "hi", forward)
            partner_out = lax.ppermute(partner_out, "hi", backward)
        own_at = 2 * order_table[(here - step) % n_hi] + half
        partner_at = 2 * order_table[(here + step) % n_hi] + other
        gathered_w = store(gathered_w, own_piece, own_at)
        gathered_w = store(gathered_w, partner_piece, partner_at)
        gathered_o = store_out(gathered_o, own_out, own_at)
        gathered_o = store_out(gathered_o, partner_out, partner_at)
    o_full = gathered_o.reshape(half_width, n_ctx * e_cols)

    projected = jnp.dot(
        normed,
        gathered_w.reshape(n_ctx * w_rows, 3 * half_width),
        preferred_element_type=jnp.float32,
    )
    projected = projected.astype(jnp.bfloat16).reshape(row_count, 3, half_width)

    taps = half_of(short_filter, 2, half)
    prior_rows = shifted(projected[row_count - (short_taps - 1) :], "hi", 1)
    featured = featurize(jnp.concatenate([prior_rows, projected], axis=0), taps, row_count)
    mixed = (featured[:, 1] * featured[:, 2]).astype(jnp.bfloat16)
    mixed_prior = shifted(mixed[row_count - (filter_len - 1) :], "hi", 1)
    query = featured[:, 0]
    zero_row = jnp.zeros((1, half_width), jnp.bfloat16)
    extended_mix = jnp.concatenate([zero_row, mixed_prior, mixed], axis=0)
    groups_here = long_filter.shape[1] // 2
    group_size = half_width // groups_here
    mix_blocks = extended_mix.reshape(
        row_count // filter_len + 1, filter_len, groups_here, group_size
    )
    filtered = jnp.einsum(
        "gts,bsgc->btgc", current, mix_blocks[1:], preferred_element_type=jnp.float32
    )
    filtered = filtered + jnp.einsum(
        "gts,bsgc->btgc", previous, mix_blocks[:-1], preferred_element_type=jnp.float32
    )
    gated = (query * filtered.reshape(row_count, half_width)).astype(jnp.bfloat16)

    def out_terms(rows):
        terms = jnp.dot(rows, o_full, preferred_element_type=jnp.float32).astype(jnp.bfloat16)
        return lax.psum_scatter(terms, "tp", scatter_dimension=1, tiled=True)

    arrived = swap_pair(out_terms(half_of(gated, 0, other)))
    summed = out_terms(half_of(gated, 0, half)).astype(jnp.float32) + arrived.astype(jnp.float32)
    return (tokens.astype(jnp.float32) + summed).astype(jnp.bfloat16)


def solution(mesh):
    n_ctx, n_tp = mesh.devices.shape
    paired = Mesh(mesh.devices.reshape(n_ctx // 2, 2, n_tp), ("hi", "lo", "tp"))
    ctx = ("hi", "lo")
    placed = (
        P(ctx, "tp"),
        P(),
        P(ctx, None, "tp"),
        P(None, None, "tp"),
        P(None, "tp"),
        P("tp", ctx),
    )
    return jax.shard_map(
        local, mesh=paired, in_specs=placed, out_specs=P(ctx, "tp"), check_vma=False
    )
```

```python
import jax
import jax.numpy as jnp
from jax import lax
from jax.sharding import Mesh
from jax.sharding import PartitionSpec as P


def shifted(value, axis, steps):
    count = lax.axis_size(axis)
    first, last = (max(0, -steps), min(count, count - steps))
    return lax.ppermute(value, axis, [(source, source + steps) for source in range(first, last)])


def swap_pair(value):
    return lax.ppermute(value, "lo", [(0, 1), (1, 0)])


def toeplitz_pair(long_filter):
    filter_len = long_filter.shape[0]
    tap = lax.broadcasted_iota(jnp.int32, (filter_len, filter_len, filter_len), 0)
    offset = lax.broadcasted_iota(jnp.int32, (filter_len, filter_len, filter_len), 1) - (
        lax.broadcasted_iota(jnp.int32, (filter_len, filter_len, filter_len), 2)
    )
    table = long_filter.T

    def spread(hot):
        return jnp.einsum("gm,mts->gts", table, hot.astype(table.dtype))

    return (spread(offset == tap), spread(offset + filter_len == tap))


def featurize(extended, short_filter, count):
    short_taps = short_filter.shape[0]
    ext_float = extended.astype(jnp.float32)
    featured = jnp.zeros((count,) + extended.shape[1:], jnp.float32)
    for tap in range(short_taps):
        featured = (
            featured
            + short_filter[tap] * ext_float[short_taps - 1 - tap : short_taps - 1 - tap + count]
        )
    return featured


def half_of(value, axis, half):
    size = value.shape[axis] // 2
    return lax.dynamic_slice_in_dim(value, half * size, size, axis)


def pair_ordered(mine, theirs, half, axis):
    first = jnp.where(half == 0, mine, theirs)
    second = jnp.where(half == 0, theirs, mine)
    return jnp.concatenate([first, second], axis=axis)


def ring_order(count):
    return list(range(0, count, 2)) + list(range(count - 1 - count % 2, 0, -2))


def local(tokens, norm_gain, w_in, short_filter, long_filter, w_out):
    own_rows, local_width = tokens.shape
    n_tp = lax.axis_size("tp")
    n_hi = lax.axis_size("hi")
    model_width = local_width * n_tp
    short_taps = short_filter.shape[0]
    filter_len = long_filter.shape[0]
    w_rows = w_in.shape[0]
    half = lax.axis_index("lo")
    other = 1 - half
    half_width = local_width // 2

    pair_tokens = pair_ordered(tokens, swap_pair(tokens), half, 0)
    pair_tokens = lax.all_gather(pair_tokens, "tp", axis=1, tiled=True)
    row_count = pair_tokens.shape[0]
    wide_float = pair_tokens.astype(jnp.float32)
    scale = lax.rsqrt(jnp.mean(wide_float * wide_float, axis=-1, keepdims=True) + 1e-06)
    normed = (wide_float * scale * norm_gain).astype(jnp.bfloat16)

    own_piece = half_of(w_in, 2, half).reshape(w_rows, 3 * half_width)
    partner_piece = swap_pair(half_of(w_in, 2, other)).reshape(w_rows, 3 * half_width)
    order = ring_order(n_hi)
    place = [0] * n_hi
    for index, member in enumerate(order):
        place[member] = index
    order_table = jnp.array(order, jnp.int32)
    here = jnp.array(place, jnp.int32)[lax.axis_index("hi")]
    forward = [(order[i], order[(i + 1) % n_hi]) for i in range(n_hi)]
    backward = [(order[(i + 1) % n_hi], order[i]) for i in range(n_hi)]

    e_cols = w_out.shape[1]
    own_out = half_of(w_out, 0, half)
    partner_out = swap_pair(half_of(w_out, 0, other))

    n_ctx = 2 * n_hi
    gathered_w = jnp.zeros((n_ctx, w_rows, 3 * half_width), jnp.bfloat16)
    gathered_o = jnp.zeros((half_width, n_ctx, e_cols), jnp.bfloat16)

    def store(buffer, piece, ctx_index):
        return lax.dynamic_update_slice_in_dim(buffer, piece[None], ctx_index, axis=0)

    def store_out(buffer, piece, ctx_index):
        return lax.dynamic_update_slice_in_dim(buffer, piece[:, None], ctx_index, axis=1)

    current, previous = toeplitz_pair(half_of(long_filter, 1, half))
    for step in range(n_hi):
        if step > 0:
            own_piece = lax.ppermute(own_piece, "hi", forward)
            partner_piece = lax.ppermute(partner_piece, "hi", backward)
            own_out = lax.ppermute(own_out, "hi", forward)
            partner_out = lax.ppermute(partner_out, "hi", backward)
        own_at = 2 * order_table[(here - step) % n_hi] + half
        partner_at = 2 * order_table[(here + step) % n_hi] + other
        gathered_w = store(gathered_w, own_piece, own_at)
        gathered_w = store(gathered_w, partner_piece, partner_at)
        gathered_o = store_out(gathered_o, own_out, own_at)
        gathered_o = store_out(gathered_o, partner_out, partner_at)
    o_full = gathered_o.reshape(half_width, n_ctx * e_cols)

    projected = jnp.dot(
        normed,
        gathered_w.reshape(n_ctx * w_rows, 3 * half_width),
        preferred_element_type=jnp.float32,
    )
    projected = projected.astype(jnp.bfloat16).reshape(row_count, 3, half_width)

    taps = half_of(short_filter, 2, half)
    prior_rows = shifted(projected[row_count - (short_taps - 1) :], "hi", 1)
    featured = featurize(jnp.concatenate([prior_rows, projected], axis=0), taps, row_count)
    mixed = (featured[:, 1] * featured[:, 2]).astype(jnp.bfloat16)
    mixed_prior = shifted(mixed[row_count - (filter_len - 1) :], "hi", 1)
    query = featured[:, 0]
    zero_row = jnp.zeros((1, half_width), jnp.bfloat16)
    extended_mix = jnp.concatenate([zero_row, mixed_prior, mixed], axis=0)
    groups_here = long_filter.shape[1] // 2
    group_size = half_width // groups_here
    mix_blocks = extended_mix.reshape(
        row_count // filter_len + 1, filter_len, groups_here, group_size
    )
    filtered = jnp.einsum(
        "gts,bsgc->btgc", current, mix_blocks[1:], preferred_element_type=jnp.float32
    )
    filtered = filtered + jnp.einsum(
        "gts,bsgc->btgc", previous, mix_blocks[:-1], preferred_element_type=jnp.float32
    )
    gated = (query * filtered.reshape(row_count, half_width)).astype(jnp.bfloat16)

    def out_terms(rows):
        terms = jnp.dot(rows, o_full, preferred_element_type=jnp.float32).astype(jnp.bfloat16)
        return lax.psum_scatter(terms, "tp", scatter_dimension=1, tiled=True)

    arrived = swap_pair(out_terms(half_of(gated, 0, other)))
    summed = out_terms(half_of(gated, 0, half)).astype(jnp.float32) + arrived.astype(jnp.float32)
    return (tokens.astype(jnp.float32) + summed).astype(jnp.bfloat16)


def solution(mesh):
    n_ctx, n_tp = mesh.devices.shape
    paired = Mesh(mesh.devices.reshape(n_ctx // 2, 2, n_tp), ("hi", "lo", "tp"))
    ctx = ("hi", "lo")
    placed = (
        P(ctx, "tp"),
        P(),
        P(ctx, None, "tp"),
        P(None, None, "tp"),
        P(None, "tp"),
        P("tp", ctx),
    )
    return jax.shard_map(
        local, mesh=paired, in_specs=placed, out_specs=P(ctx, "tp"), check_vma=False
    )
```

```python
import jax
import jax.numpy as jnp
from jax import lax
from jax.sharding import Mesh
from jax.sharding import PartitionSpec as P


def shifted(value, axis, steps):
    count = lax.axis_size(axis)
    first, last = (max(0, -steps), min(count, count - steps))
    return lax.ppermute(value, axis, [(source, source + steps) for source in range(first, last)])


def swap_pair(value):
    return lax.ppermute(value, "lo", [(0, 1), (1, 0)])


def toeplitz_pair(long_filter):
    filter_len = long_filter.shape[0]
    tap = lax.broadcasted_iota(jnp.int32, (filter_len, filter_len, filter_len), 0)
    offset = lax.broadcasted_iota(jnp.int32, (filter_len, filter_len, filter_len), 1) - (
        lax.broadcasted_iota(jnp.int32, (filter_len, filter_len, filter_len), 2)
    )
    table = long_filter.T

    def spread(hot):
        return jnp.einsum("gm,mts->gts", table, hot.astype(table.dtype))

    return (spread(offset == tap), spread(offset + filter_len == tap))


def featurize(extended, short_filter, count):
    short_taps = short_filter.shape[0]
    ext_float = extended.astype(jnp.float32)
    featured = jnp.zeros((count,) + extended.shape[1:], jnp.float32)
    for tap in range(short_taps):
        featured = (
            featured
            + short_filter[tap] * ext_float[short_taps - 1 - tap : short_taps - 1 - tap + count]
        )
    return featured


def half_of(value, axis, half):
    size = value.shape[axis] // 2
    return lax.dynamic_slice_in_dim(value, half * size, size, axis)


def pair_ordered(mine, theirs, half, axis):
    first = jnp.where(half == 0, mine, theirs)
    second = jnp.where(half == 0, theirs, mine)
    return jnp.concatenate([first, second], axis=axis)


def ring_order(count):
    return list(range(0, count, 2)) + list(range(count - 1 - count % 2, 0, -2))


def local(tokens, norm_gain, w_in, short_filter, long_filter, w_out):
    own_rows, local_width = tokens.shape
    n_tp = lax.axis_size("tp")
    n_hi = lax.axis_size("hi")
    model_width = local_width * n_tp
    short_taps = short_filter.shape[0]
    filter_len = long_filter.shape[0]
    w_rows = w_in.shape[0]
    half = lax.axis_index("lo")
    other = 1 - half
    half_width = local_width // 2

    pair_tokens = pair_ordered(tokens, swap_pair(tokens), half, 0)
    pair_tokens = lax.all_gather(pair_tokens, "tp", axis=1, tiled=True)
    row_count = pair_tokens.shape[0]
    wide_float = pair_tokens.astype(jnp.float32)
    scale = lax.rsqrt(jnp.mean(wide_float * wide_float, axis=-1, keepdims=True) + 1e-06)
    normed = (wide_float * scale * norm_gain).astype(jnp.bfloat16)

    own_piece = half_of(w_in, 2, half).reshape(w_rows, 3 * half_width)
    partner_piece = swap_pair(half_of(w_in, 2, other)).reshape(w_rows, 3 * half_width)
    order = ring_order(n_hi)
    place = [0] * n_hi
    for index, member in enumerate(order):
        place[member] = index
    order_table = jnp.array(order, jnp.int32)
    here = jnp.array(place, jnp.int32)[lax.axis_index("hi")]
    forward = [(order[i], order[(i + 1) % n_hi]) for i in range(n_hi)]
    backward = [(order[(i + 1) % n_hi], order[i]) for i in range(n_hi)]

    e_cols = w_out.shape[1]
    own_out = half_of(w_out, 0, half)
    partner_out = swap_pair(half_of(w_out, 0, other))

    n_ctx = 2 * n_hi
    gathered_w = jnp.zeros((n_ctx, w_rows, 3 * half_width), jnp.bfloat16)
    gathered_o = jnp.zeros((half_width, n_ctx, e_cols), jnp.bfloat16)

    def store(buffer, piece, ctx_index):
        return lax.dynamic_update_slice_in_dim(buffer, piece[None], ctx_index, axis=0)

    def store_out(buffer, piece, ctx_index):
        return lax.dynamic_update_slice_in_dim(buffer, piece[:, None], ctx_index, axis=1)

    current, previous = toeplitz_pair(half_of(long_filter, 1, half))
    for step in range(n_hi):
        if step > 0:
            own_piece = lax.ppermute(own_piece, "hi", forward)
            partner_piece = lax.ppermute(partner_piece, "hi", backward)
            own_out = lax.ppermute(own_out, "hi", forward)
            partner_out = lax.ppermute(partner_out, "hi", backward)
        own_at = 2 * order_table[(here - step) % n_hi] + half
        partner_at = 2 * order_table[(here + step) % n_hi] + other
        gathered_w = store(gathered_w, own_piece, own_at)
        gathered_w = store(gathered_w, partner_piece, partner_at)
        gathered_o = store_out(gathered_o, own_out, own_at)
        gathered_o = store_out(gathered_o, partner_out, partner_at)
    o_full = gathered_o.reshape(half_width, n_ctx * e_cols)

    projected = jnp.dot(
        normed,
        gathered_w.reshape(n_ctx * w_rows, 3 * half_width),
        preferred_element_type=jnp.float32,
    )
    projected = projected.astype(jnp.bfloat16).reshape(row_count, 3, half_width)

    taps = half_of(short_filter, 2, half)
    prior_rows = shifted(projected[row_count - (short_taps - 1) :], "hi", 1)
    featured = featurize(jnp.concatenate([prior_rows, projected], axis=0), taps, row_count)
    mixed = (featured[:, 1] * featured[:, 2]).astype(jnp.bfloat16)
    mixed_prior = shifted(mixed[row_count - (filter_len - 1) :], "hi", 1)
    query = featured[:, 0]
    zero_row = jnp.zeros((1, half_width), jnp.bfloat16)
    extended_mix = jnp.concatenate([zero_row, mixed_prior, mixed], axis=0)
    groups_here = long_filter.shape[1] // 2
    group_size = half_width // groups_here
    block_count = own_rows // filter_len

    def gated_rows(part):
        window = lax.dynamic_slice_in_dim(extended_mix, part * own_rows, own_rows + filter_len, 0)
        mix_blocks = window.reshape(block_count + 1, filter_len, groups_here, group_size)
        filtered = jnp.einsum(
            "gts,bsgc->btgc", current, mix_blocks[1:], preferred_element_type=jnp.float32
        )
        filtered = filtered + jnp.einsum(
            "gts,bsgc->btgc", previous, mix_blocks[:-1], preferred_element_type=jnp.float32
        )
        rows = lax.dynamic_slice_in_dim(query, part * own_rows, own_rows, 0)
        return (rows * filtered.reshape(own_rows, half_width)).astype(jnp.bfloat16)

    def out_terms(rows):
        terms = jnp.dot(rows, o_full, preferred_element_type=jnp.float32).astype(jnp.bfloat16)
        return lax.psum_scatter(terms, "tp", scatter_dimension=1, tiled=True)

    arrived = swap_pair(out_terms(gated_rows(other)))
    summed = out_terms(gated_rows(half)).astype(jnp.float32) + arrived.astype(jnp.float32)
    return (tokens.astype(jnp.float32) + summed).astype(jnp.bfloat16)


def solution(mesh):
    n_ctx, n_tp = mesh.devices.shape
    paired = Mesh(mesh.devices.reshape(n_ctx // 2, 2, n_tp), ("hi", "lo", "tp"))
    ctx = ("hi", "lo")
    placed = (
        P(ctx, "tp"),
        P(),
        P(ctx, None, "tp"),
        P(None, None, "tp"),
        P(None, "tp"),
        P("tp", ctx),
    )
    return jax.shard_map(
        local, mesh=paired, in_specs=placed, out_specs=P(ctx, "tp"), check_vma=False
    )
```

```python
import jax
import jax.numpy as jnp
from jax import lax
from jax.sharding import Mesh
from jax.sharding import PartitionSpec as P


def shifted(value, axis, steps):
    count = lax.axis_size(axis)
    first, last = (max(0, -steps), min(count, count - steps))
    return lax.ppermute(value, axis, [(source, source + steps) for source in range(first, last)])


def swap_pair(value):
    return lax.ppermute(value, "lo", [(0, 1), (1, 0)])


def toeplitz_pair(long_filter):
    filter_len = long_filter.shape[0]
    tap = lax.broadcasted_iota(jnp.int32, (filter_len, filter_len, filter_len), 0)
    offset = lax.broadcasted_iota(jnp.int32, (filter_len, filter_len, filter_len), 1) - (
        lax.broadcasted_iota(jnp.int32, (filter_len, filter_len, filter_len), 2)
    )
    table = long_filter.T

    def spread(hot):
        return jnp.einsum("gm,mts->gts", table, hot.astype(table.dtype))

    return (spread(offset == tap), spread(offset + filter_len == tap))


def featurize(extended, short_filter, count):
    short_taps = short_filter.shape[0]
    ext_float = extended.astype(jnp.float32)
    featured = jnp.zeros((count,) + extended.shape[1:], jnp.float32)
    for tap in range(short_taps):
        featured = (
            featured
            + short_filter[tap] * ext_float[short_taps - 1 - tap : short_taps - 1 - tap + count]
        )
    return featured


def half_of(value, axis, half):
    size = value.shape[axis] // 2
    return lax.dynamic_slice_in_dim(value, half * size, size, axis)


def pair_ordered(mine, theirs, half, axis):
    first = jnp.where(half == 0, mine, theirs)
    second = jnp.where(half == 0, theirs, mine)
    return jnp.concatenate([first, second], axis=axis)


def ring_order(count):
    return list(range(0, count, 2)) + list(range(count - 1 - count % 2, 0, -2))


def local(tokens, norm_gain, w_in, short_filter, long_filter, w_out):
    own_rows, local_width = tokens.shape
    n_tp = lax.axis_size("tp")
    n_hi = lax.axis_size("hi")
    model_width = local_width * n_tp
    short_taps = short_filter.shape[0]
    filter_len = long_filter.shape[0]
    w_rows = w_in.shape[0]
    half = lax.axis_index("lo")
    other = 1 - half
    half_width = local_width // 2

    own_piece = half_of(w_in, 2, half).reshape(w_rows, 3 * half_width)
    partner_piece = swap_pair(half_of(w_in, 2, other)).reshape(w_rows, 3 * half_width)
    order = ring_order(n_hi)
    place = [0] * n_hi
    for index, member in enumerate(order):
        place[member] = index
    order_table = jnp.array(order, jnp.int32)
    here = jnp.array(place, jnp.int32)[lax.axis_index("hi")]
    forward = [(order[i], order[(i + 1) % n_hi]) for i in range(n_hi)]
    backward = [(order[(i + 1) % n_hi], order[i]) for i in range(n_hi)]

    e_cols = w_out.shape[1]
    own_out = half_of(w_out, 0, half)
    partner_out = swap_pair(half_of(w_out, 0, other))

    n_ctx = 2 * n_hi
    gathered_w = jnp.zeros((n_ctx, w_rows, 3 * half_width), jnp.bfloat16)
    gathered_o = jnp.zeros((half_width, n_ctx, e_cols), jnp.bfloat16)

    def store(buffer, piece, ctx_index):
        return lax.dynamic_update_slice_in_dim(buffer, piece[None], ctx_index, axis=0)

    def store_out(buffer, piece, ctx_index):
        return lax.dynamic_update_slice_in_dim(buffer, piece[:, None], ctx_index, axis=1)

    current, previous = toeplitz_pair(half_of(long_filter, 1, half))
    late = min(2, n_hi - 1)
    late_w = []
    late_columns = []
    for step in range(n_hi):
        if step > 0:
            own_piece = lax.ppermute(own_piece, "hi", forward)
            partner_piece = lax.ppermute(partner_piece, "hi", backward)
            own_out = lax.ppermute(own_out, "hi", forward)
            partner_out = lax.ppermute(partner_out, "hi", backward)
        own_at = 2 * order_table[(here - step) % n_hi] + half
        partner_at = 2 * order_table[(here + step) % n_hi] + other
        if step < n_hi - late:
            gathered_w = store(gathered_w, own_piece, own_at)
            gathered_w = store(gathered_w, partner_piece, partner_at)
        else:
            late_w += [own_piece, partner_piece]
            late_columns += [own_at, partner_at]
        gathered_o = store_out(gathered_o, own_out, own_at)
        gathered_o = store_out(gathered_o, partner_out, partner_at)
    o_full = gathered_o.reshape(half_width, n_ctx * e_cols)

    pair_tokens = pair_ordered(tokens, swap_pair(tokens), half, 0)
    pair_tokens = lax.all_gather(pair_tokens, "tp", axis=1, tiled=True)
    row_count = pair_tokens.shape[0]
    wide_float = pair_tokens.astype(jnp.float32)
    scale = lax.rsqrt(jnp.mean(wide_float * wide_float, axis=-1, keepdims=True) + 1e-06)
    normed = (wide_float * scale * norm_gain).astype(jnp.bfloat16)

    early_part = jnp.dot(
        normed,
        gathered_w.reshape(n_ctx * w_rows, 3 * half_width),
        preferred_element_type=jnp.float32,
    )
    late_normed = jnp.concatenate(
        [lax.dynamic_slice_in_dim(normed, at * w_rows, w_rows, axis=1) for at in late_columns], axis=1
    )
    projected = early_part + jnp.dot(
        late_normed, jnp.concatenate(late_w, axis=0), preferred_element_type=jnp.float32
    )
    projected = projected.astype(jnp.bfloat16).reshape(row_count, 3, half_width)

    taps = half_of(short_filter, 2, half)
    prior_rows = shifted(projected[row_count - (short_taps - 1) :], "hi", 1)
    featured = featurize(jnp.concatenate([prior_rows, projected], axis=0), taps, row_count)
    mixed = (featured[:, 1] * featured[:, 2]).astype(jnp.bfloat16)
    mixed_prior = shifted(mixed[row_count - (filter_len - 1) :], "hi", 1)
    query = featured[:, 0]
    zero_row = jnp.zeros((1, half_width), jnp.bfloat16)
    extended_mix = jnp.concatenate([zero_row, mixed_prior, mixed], axis=0)
    groups_here = long_filter.shape[1] // 2
    group_size = half_width // groups_here
    mix_blocks = extended_mix.reshape(
        row_count // filter_len + 1, filter_len, groups_here, group_size
    )
    filtered = jnp.einsum(
        "gts,bsgc->btgc", current, mix_blocks[1:], preferred_element_type=jnp.float32
    )
    filtered = filtered + jnp.einsum(
        "gts,bsgc->btgc", previous, mix_blocks[:-1], preferred_element_type=jnp.float32
    )
    gated = (query * filtered.reshape(row_count, half_width)).astype(jnp.bfloat16)

    def out_terms(rows):
        terms = jnp.dot(rows, o_full, preferred_element_type=jnp.float32).astype(jnp.bfloat16)
        return lax.psum_scatter(terms, "tp", scatter_dimension=1, tiled=True)

    arrived = swap_pair(out_terms(half_of(gated, 0, other)))
    summed = out_terms(half_of(gated, 0, half)).astype(jnp.float32) + arrived.astype(jnp.float32)
    return (tokens.astype(jnp.float32) + summed).astype(jnp.bfloat16)


def solution(mesh):
    n_ctx, n_tp = mesh.devices.shape
    paired = Mesh(mesh.devices.reshape(n_ctx // 2, 2, n_tp), ("hi", "lo", "tp"))
    ctx = ("hi", "lo")
    placed = (
        P(ctx, "tp"),
        P(),
        P(ctx, None, "tp"),
        P(None, None, "tp"),
        P(None, "tp"),
        P("tp", ctx),
    )
    return jax.shard_map(
        local, mesh=paired, in_specs=placed, out_specs=P(ctx, "tp"), check_vma=False
    )
```

```python
import jax
import jax.numpy as jnp
from jax import lax
from jax.sharding import Mesh
from jax.sharding import PartitionSpec as P


def shifted(value, axis, steps):
    count = lax.axis_size(axis)
    first, last = (max(0, -steps), min(count, count - steps))
    return lax.ppermute(value, axis, [(source, source + steps) for source in range(first, last)])


def swap_pair(value):
    return lax.ppermute(value, "lo", [(0, 1), (1, 0)])


def toeplitz_pair(long_filter):
    filter_len = long_filter.shape[0]
    tap = lax.broadcasted_iota(jnp.int32, (filter_len, filter_len, filter_len), 0)
    offset = lax.broadcasted_iota(jnp.int32, (filter_len, filter_len, filter_len), 1) - (
        lax.broadcasted_iota(jnp.int32, (filter_len, filter_len, filter_len), 2)
    )
    table = long_filter.T

    def spread(hot):
        return jnp.einsum("gm,mts->gts", table, hot.astype(table.dtype))

    return (spread(offset == tap), spread(offset + filter_len == tap))


def featurize(extended, short_filter, count):
    short_taps = short_filter.shape[0]
    ext_float = extended.astype(jnp.float32)
    featured = jnp.zeros((count,) + extended.shape[1:], jnp.float32)
    for tap in range(short_taps):
        featured = (
            featured
            + short_filter[tap] * ext_float[short_taps - 1 - tap : short_taps - 1 - tap + count]
        )
    return featured


def half_of(value, axis, half):
    size = value.shape[axis] // 2
    return lax.dynamic_slice_in_dim(value, half * size, size, axis)


def pair_ordered(mine, theirs, half, axis):
    first = jnp.where(half == 0, mine, theirs)
    second = jnp.where(half == 0, theirs, mine)
    return jnp.concatenate([first, second], axis=axis)


def ring_order(count):
    return list(range(0, count, 2)) + list(range(count - 1 - count % 2, 0, -2))


def local(tokens, norm_gain, w_in, short_filter, long_filter, w_out):
    own_rows, local_width = tokens.shape
    n_tp = lax.axis_size("tp")
    n_hi = lax.axis_size("hi")
    model_width = local_width * n_tp
    short_taps = short_filter.shape[0]
    filter_len = long_filter.shape[0]
    w_rows = w_in.shape[0]
    half = lax.axis_index("lo")
    other = 1 - half
    half_width = local_width // 2

    own_piece = half_of(w_in, 2, half).reshape(w_rows, 3 * half_width)
    partner_piece = swap_pair(half_of(w_in, 2, other)).reshape(w_rows, 3 * half_width)
    order = ring_order(n_hi)
    place = [0] * n_hi
    for index, member in enumerate(order):
        place[member] = index
    order_table = jnp.array(order, jnp.int32)
    here = jnp.array(place, jnp.int32)[lax.axis_index("hi")]
    forward = [(order[i], order[(i + 1) % n_hi]) for i in range(n_hi)]
    backward = [(order[(i + 1) % n_hi], order[i]) for i in range(n_hi)]

    e_cols = w_out.shape[1]
    own_out = half_of(w_out, 0, half)
    partner_out = swap_pair(half_of(w_out, 0, other))

    n_ctx = 2 * n_hi
    gathered_w = jnp.zeros((n_ctx, w_rows, 3 * half_width), jnp.bfloat16)
    gathered_o = jnp.zeros((half_width, n_ctx, e_cols), jnp.bfloat16)

    def store(buffer, piece, ctx_index):
        return lax.dynamic_update_slice_in_dim(buffer, piece[None], ctx_index, axis=0)

    def store_out(buffer, piece, ctx_index):
        return lax.dynamic_update_slice_in_dim(buffer, piece[:, None], ctx_index, axis=1)

    current, previous = toeplitz_pair(half_of(long_filter, 1, half))
    chunks = max(c for c in range(1, min(n_hi - 1, 6) + 1) if own_rows % c == 0)
    chunk_rows = own_rows // chunks
    arrived_tokens = []
    for step in range(n_hi):
        if 0 < step <= chunks:
            sending, own_piece = lax.optimization_barrier(
                (tokens[(step - 1) * chunk_rows : step * chunk_rows], own_piece)
            )
            arrived_tokens.append(swap_pair(sending))
        if step > 0:
            own_piece = lax.ppermute(own_piece, "hi", forward)
            partner_piece = lax.ppermute(partner_piece, "hi", backward)
            own_out = lax.ppermute(own_out, "hi", forward)
            partner_out = lax.ppermute(partner_out, "hi", backward)
        own_at = 2 * order_table[(here - step) % n_hi] + half
        partner_at = 2 * order_table[(here + step) % n_hi] + other
        gathered_w = store(gathered_w, own_piece, own_at)
        gathered_w = store(gathered_w, partner_piece, partner_at)
        gathered_o = store_out(gathered_o, own_out, own_at)
        gathered_o = store_out(gathered_o, partner_out, partner_at)
    o_full = gathered_o.reshape(half_width, n_ctx * e_cols)

    pair_tokens = pair_ordered(tokens, jnp.concatenate(arrived_tokens, axis=0), half, 0)
    pair_tokens = lax.all_gather(pair_tokens, "tp", axis=1, tiled=True)
    row_count = pair_tokens.shape[0]
    wide_float = pair_tokens.astype(jnp.float32)
    scale = lax.rsqrt(jnp.mean(wide_float * wide_float, axis=-1, keepdims=True) + 1e-06)
    normed = (wide_float * scale * norm_gain).astype(jnp.bfloat16)


    projected = jnp.dot(
        normed,
        gathered_w.reshape(n_ctx * w_rows, 3 * half_width),
        preferred_element_type=jnp.float32,
    )
    projected = projected.astype(jnp.bfloat16).reshape(row_count, 3, half_width)

    taps = half_of(short_filter, 2, half)
    prior_rows = shifted(projected[row_count - (short_taps - 1) :], "hi", 1)
    featured = featurize(jnp.concatenate([prior_rows, projected], axis=0), taps, row_count)
    mixed = (featured[:, 1] * featured[:, 2]).astype(jnp.bfloat16)
    mixed_prior = shifted(mixed[row_count - (filter_len - 1) :], "hi", 1)
    query = featured[:, 0]
    zero_row = jnp.zeros((1, half_width), jnp.bfloat16)
    extended_mix = jnp.concatenate([zero_row, mixed_prior, mixed], axis=0)
    groups_here = long_filter.shape[1] // 2
    group_size = half_width // groups_here
    mix_blocks = extended_mix.reshape(
        row_count // filter_len + 1, filter_len, groups_here, group_size
    )
    filtered = jnp.einsum(
        "gts,bsgc->btgc", current, mix_blocks[1:], preferred_element_type=jnp.float32
    )
    filtered = filtered + jnp.einsum(
        "gts,bsgc->btgc", previous, mix_blocks[:-1], preferred_element_type=jnp.float32
    )
    gated = (query * filtered.reshape(row_count, half_width)).astype(jnp.bfloat16)

    def out_terms(rows):
        terms = jnp.dot(rows, o_full, preferred_element_type=jnp.float32).astype(jnp.bfloat16)
        return lax.psum_scatter(terms, "tp", scatter_dimension=1, tiled=True)

    arrived = swap_pair(out_terms(half_of(gated, 0, other)))
    summed = out_terms(half_of(gated, 0, half)).astype(jnp.float32) + arrived.astype(jnp.float32)
    return (tokens.astype(jnp.float32) + summed).astype(jnp.bfloat16)


def solution(mesh):
    n_ctx, n_tp = mesh.devices.shape
    paired = Mesh(mesh.devices.reshape(n_ctx // 2, 2, n_tp), ("hi", "lo", "tp"))
    ctx = ("hi", "lo")
    placed = (
        P(ctx, "tp"),
        P(),
        P(ctx, None, "tp"),
        P(None, None, "tp"),
        P(None, "tp"),
        P("tp", ctx),
    )
    return jax.shard_map(
        local, mesh=paired, in_specs=placed, out_specs=P(ctx, "tp"), check_vma=False
    )
```

```python
import jax
import jax.numpy as jnp
from jax import lax
from jax.sharding import Mesh
from jax.sharding import PartitionSpec as P


def shifted(value, axis, steps):
    count = lax.axis_size(axis)
    first, last = (max(0, -steps), min(count, count - steps))
    return lax.ppermute(value, axis, [(source, source + steps) for source in range(first, last)])


def swap_pair(value):
    return lax.ppermute(value, "lo", [(0, 1), (1, 0)])


def toeplitz_pair(long_filter):
    filter_len = long_filter.shape[0]
    tap = lax.broadcasted_iota(jnp.int32, (filter_len, filter_len, filter_len), 0)
    offset = lax.broadcasted_iota(jnp.int32, (filter_len, filter_len, filter_len), 1) - (
        lax.broadcasted_iota(jnp.int32, (filter_len, filter_len, filter_len), 2)
    )
    table = long_filter.T

    def spread(hot):
        return jnp.einsum("gm,mts->gts", table, hot.astype(table.dtype))

    return (spread(offset == tap), spread(offset + filter_len == tap))


def half_of(value, axis, half):
    size = value.shape[axis] // 2
    return lax.dynamic_slice_in_dim(value, half * size, size, axis)


def pair_ordered(mine, theirs, half, axis):
    first = jnp.where(half == 0, mine, theirs)
    second = jnp.where(half == 0, theirs, mine)
    return jnp.concatenate([first, second], axis=axis)


def ring_order(count):
    return list(range(0, count, 2)) + list(range(count - 1 - count % 2, 0, -2))


def local(tokens, norm_gain, w_in, short_filter, long_filter, w_out):
    own_rows, local_width = tokens.shape
    n_tp = lax.axis_size("tp")
    n_hi = lax.axis_size("hi")
    model_width = local_width * n_tp
    short_taps = short_filter.shape[0]
    filter_len = long_filter.shape[0]
    w_rows = w_in.shape[0]
    half = lax.axis_index("lo")
    other = 1 - half
    half_width = local_width // 2

    pair_tokens = pair_ordered(tokens, swap_pair(tokens), half, 0)
    pair_tokens = lax.all_gather(pair_tokens, "tp", axis=1, tiled=True)
    row_count = pair_tokens.shape[0]
    wide_float = pair_tokens.astype(jnp.float32)
    scale = lax.rsqrt(jnp.mean(wide_float * wide_float, axis=-1, keepdims=True) + 1e-06)
    normed = (wide_float * scale * norm_gain).astype(jnp.bfloat16)

    own_piece = half_of(w_in, 2, half).reshape(w_rows, 3 * half_width)
    partner_piece = swap_pair(half_of(w_in, 2, other)).reshape(w_rows, 3 * half_width)
    order = ring_order(n_hi)
    place = [0] * n_hi
    for index, member in enumerate(order):
        place[member] = index
    order_table = jnp.array(order, jnp.int32)
    here = jnp.array(place, jnp.int32)[lax.axis_index("hi")]
    forward = [(order[i], order[(i + 1) % n_hi]) for i in range(n_hi)]
    backward = [(order[(i + 1) % n_hi], order[i]) for i in range(n_hi)]

    e_cols = w_out.shape[1]
    own_out = half_of(w_out, 0, half)
    partner_out = swap_pair(half_of(w_out, 0, other))

    n_ctx = 2 * n_hi
    gathered_w = jnp.zeros((n_ctx, w_rows, 3 * half_width), jnp.bfloat16)
    gathered_o = jnp.zeros((half_width, n_ctx, e_cols), jnp.bfloat16)

    def store(buffer, piece, ctx_index):
        return lax.dynamic_update_slice_in_dim(buffer, piece[None], ctx_index, axis=0)

    def store_out(buffer, piece, ctx_index):
        return lax.dynamic_update_slice_in_dim(buffer, piece[:, None], ctx_index, axis=1)

    current, previous = toeplitz_pair(half_of(long_filter, 1, half))
    for step in range(n_hi):
        if step > 0:
            own_piece = lax.ppermute(own_piece, "hi", forward)
            partner_piece = lax.ppermute(partner_piece, "hi", backward)
            own_out = lax.ppermute(own_out, "hi", forward)
            partner_out = lax.ppermute(partner_out, "hi", backward)
        own_at = 2 * order_table[(here - step) % n_hi] + half
        partner_at = 2 * order_table[(here + step) % n_hi] + other
        gathered_w = store(gathered_w, own_piece, own_at)
        gathered_w = store(gathered_w, partner_piece, partner_at)
        gathered_o = store_out(gathered_o, own_out, own_at)
        gathered_o = store_out(gathered_o, partner_out, partner_at)
    o_full = gathered_o.reshape(half_width, n_ctx * e_cols)

    projected = jnp.dot(
        normed,
        gathered_w.reshape(n_ctx * w_rows, 3 * half_width),
        preferred_element_type=jnp.float32,
    )
    projected = projected.astype(jnp.bfloat16).reshape(row_count, 3, half_width)

    taps = half_of(short_filter, 2, half)
    prior_rows = shifted(projected[row_count - (short_taps - 1) :], "hi", 1)
    extended = jnp.concatenate([prior_rows, projected], axis=0)

    def stream(index):
        featured = jnp.zeros((row_count, half_width), jnp.float32)
        for tap in range(short_taps):
            rows = extended[short_taps - 1 - tap : short_taps - 1 - tap + row_count, index]
            featured = featured + taps[tap, index] * rows.astype(jnp.float32)
        return featured

    mixed = (stream(1) * stream(2)).astype(jnp.bfloat16)
    mixed_prior = shifted(mixed[row_count - (filter_len - 1) :], "hi", 1)
    query = stream(0)
    zero_row = jnp.zeros((1, half_width), jnp.bfloat16)
    extended_mix = jnp.concatenate([zero_row, mixed_prior, mixed], axis=0)
    groups_here = long_filter.shape[1] // 2
    group_size = half_width // groups_here
    mix_blocks = extended_mix.reshape(
        row_count // filter_len + 1, filter_len, groups_here, group_size
    )
    filtered = jnp.einsum(
        "gts,bsgc->btgc", current, mix_blocks[1:], preferred_element_type=jnp.float32
    )
    filtered = filtered + jnp.einsum(
        "gts,bsgc->btgc", previous, mix_blocks[:-1], preferred_element_type=jnp.float32
    )
    gated = (query * filtered.reshape(row_count, half_width)).astype(jnp.bfloat16)

    def out_terms(rows):
        terms = jnp.dot(rows, o_full, preferred_element_type=jnp.float32).astype(jnp.bfloat16)
        return lax.psum_scatter(terms, "tp", scatter_dimension=1, tiled=True)

    arrived = swap_pair(out_terms(half_of(gated, 0, other)))
    summed = out_terms(half_of(gated, 0, half)).astype(jnp.float32) + arrived.astype(jnp.float32)
    return (tokens.astype(jnp.float32) + summed).astype(jnp.bfloat16)


def solution(mesh):
    n_ctx, n_tp = mesh.devices.shape
    paired = Mesh(mesh.devices.reshape(n_ctx // 2, 2, n_tp), ("hi", "lo", "tp"))
    ctx = ("hi", "lo")
    placed = (
        P(ctx, "tp"),
        P(),
        P(ctx, None, "tp"),
        P(None, None, "tp"),
        P(None, "tp"),
        P("tp", ctx),
    )
    return jax.shard_map(
        local, mesh=paired, in_specs=placed, out_specs=P(ctx, "tp"), check_vma=False
    )
```

```python
import jax
import jax.numpy as jnp
from jax import lax
from jax.sharding import Mesh
from jax.sharding import PartitionSpec as P


def shifted(value, axis, steps):
    count = lax.axis_size(axis)
    first, last = (max(0, -steps), min(count, count - steps))
    return lax.ppermute(value, axis, [(source, source + steps) for source in range(first, last)])


def swap_pair(value):
    return lax.ppermute(value, "lo", [(0, 1), (1, 0)])


def toeplitz_pair(long_filter):
    filter_len = long_filter.shape[0]
    tap = lax.broadcasted_iota(jnp.int32, (filter_len, filter_len, filter_len), 0)
    offset = lax.broadcasted_iota(jnp.int32, (filter_len, filter_len, filter_len), 1) - (
        lax.broadcasted_iota(jnp.int32, (filter_len, filter_len, filter_len), 2)
    )
    table = long_filter.T

    def spread(hot):
        return jnp.einsum("gm,mts->gts", table, hot.astype(table.dtype))

    return (spread(offset == tap), spread(offset + filter_len == tap))


def featurize(extended, short_filter, count):
    short_taps = short_filter.shape[0]
    ext_float = extended.astype(jnp.float32)
    featured = jnp.zeros((count,) + extended.shape[1:], jnp.float32)
    for tap in range(short_taps):
        featured = (
            featured
            + short_filter[tap] * ext_float[short_taps - 1 - tap : short_taps - 1 - tap + count]
        )
    return featured


def half_of(value, axis, half):
    size = value.shape[axis] // 2
    return lax.dynamic_slice_in_dim(value, half * size, size, axis)


def pair_ordered(mine, theirs, half, axis):
    first = jnp.where(half == 0, mine, theirs)
    second = jnp.where(half == 0, theirs, mine)
    return jnp.concatenate([first, second], axis=axis)


def ring_order(count):
    return list(range(0, count, 2)) + list(range(count - 1 - count % 2, 0, -2))


def local(tokens, norm_gain, w_in, short_filter, long_filter, w_out):
    own_rows, local_width = tokens.shape
    n_tp = lax.axis_size("tp")
    n_hi = lax.axis_size("hi")
    model_width = local_width * n_tp
    short_taps = short_filter.shape[0]
    filter_len = long_filter.shape[0]
    w_rows = w_in.shape[0]
    half = lax.axis_index("lo")
    other = 1 - half
    half_width = local_width // 2

    pair_tokens = pair_ordered(tokens, swap_pair(tokens), half, 0)
    pair_tokens = lax.all_gather(pair_tokens, "tp", axis=1, tiled=True)
    row_count = pair_tokens.shape[0]
    wide_float = pair_tokens.astype(jnp.float32)
    scale = lax.rsqrt(jnp.mean(wide_float * wide_float, axis=-1, keepdims=True) + 1e-06)
    normed = (wide_float * scale * norm_gain).astype(jnp.bfloat16)

    own_piece = half_of(w_in, 2, half).reshape(w_rows, 3 * half_width)
    partner_piece = swap_pair(half_of(w_in, 2, other)).reshape(w_rows, 3 * half_width)
    order = ring_order(n_hi)
    place = [0] * n_hi
    for index, member in enumerate(order):
        place[member] = index
    order_table = jnp.array(order, jnp.int32)
    here = jnp.array(place, jnp.int32)[lax.axis_index("hi")]
    forward = [(order[i], order[(i + 1) % n_hi]) for i in range(n_hi)]
    backward = [(order[(i + 1) % n_hi], order[i]) for i in range(n_hi)]

    e_cols = w_out.shape[1]
    own_out = half_of(w_out, 0, half)
    partner_out = swap_pair(half_of(w_out, 0, other))

    n_ctx = 2 * n_hi
    gathered_w = jnp.zeros((n_ctx, w_rows, 3 * half_width), jnp.bfloat16)
    gathered_o = jnp.zeros((half_width, n_ctx, e_cols), jnp.bfloat16)

    def store(buffer, piece, ctx_index):
        return lax.dynamic_update_slice_in_dim(buffer, piece[None], ctx_index, axis=0)

    def store_out(buffer, piece, ctx_index):
        return lax.dynamic_update_slice_in_dim(buffer, piece[:, None], ctx_index, axis=1)

    current, previous = toeplitz_pair(half_of(long_filter, 1, half))
    for step in range(n_hi):
        if step > 0:
            own_piece = lax.ppermute(own_piece, "hi", forward)
            partner_piece = lax.ppermute(partner_piece, "hi", backward)
            own_out = lax.ppermute(own_out, "hi", forward)
            partner_out = lax.ppermute(partner_out, "hi", backward)
        own_at = 2 * order_table[(here - step) % n_hi] + half
        partner_at = 2 * order_table[(here + step) % n_hi] + other
        gathered_w = store(gathered_w, own_piece, own_at)
        gathered_w = store(gathered_w, partner_piece, partner_at)
        gathered_o = store_out(gathered_o, own_out, own_at)
        gathered_o = store_out(gathered_o, partner_out, partner_at)
    o_full = gathered_o.reshape(half_width, n_ctx * e_cols)

    projected = jnp.dot(
        normed,
        gathered_w.reshape(n_ctx * w_rows, 3 * half_width),
        preferred_element_type=jnp.float32,
    )
    projected = projected.astype(jnp.bfloat16).reshape(row_count, 3, half_width)

    taps = half_of(short_filter, 2, half)
    prior_rows = shifted(projected[row_count - (short_taps - 1) :], "hi", 1)
    featured = featurize(jnp.concatenate([prior_rows, projected], axis=0), taps, row_count)
    mixed = (featured[:, 1] * featured[:, 2]).astype(jnp.bfloat16)
    mixed_prior = shifted(mixed[row_count - (filter_len - 1) :], "hi", 1)
    query = featured[:, 0]
    zero_row = jnp.zeros((1, half_width), jnp.bfloat16)
    groups_here = long_filter.shape[1] // 2
    group_size = half_width // groups_here
    block_shape = (filter_len, groups_here, group_size)
    mix_blocks = mixed.reshape((row_count // filter_len,) + block_shape)
    halo_block = jnp.concatenate([zero_row, mixed_prior], axis=0).reshape((1,) + block_shape)

    def apply(table, blocks):
        return jnp.einsum("gts,bsgc->btgc", table, blocks, preferred_element_type=jnp.float32)

    filtered = apply(current, mix_blocks)
    filtered = filtered + jnp.concatenate(
        [apply(previous, halo_block), apply(previous, mix_blocks[:-1])], axis=0
    )
    gated = (query * filtered.reshape(row_count, half_width)).astype(jnp.bfloat16)

    def out_terms(rows):
        terms = jnp.dot(rows, o_full, preferred_element_type=jnp.float32).astype(jnp.bfloat16)
        return lax.psum_scatter(terms, "tp", scatter_dimension=1, tiled=True)

    arrived = swap_pair(out_terms(half_of(gated, 0, other)))
    summed = out_terms(half_of(gated, 0, half)).astype(jnp.float32) + arrived.astype(jnp.float32)
    return (tokens.astype(jnp.float32) + summed).astype(jnp.bfloat16)


def solution(mesh):
    n_ctx, n_tp = mesh.devices.shape
    paired = Mesh(mesh.devices.reshape(n_ctx // 2, 2, n_tp), ("hi", "lo", "tp"))
    ctx = ("hi", "lo")
    placed = (
        P(ctx, "tp"),
        P(),
        P(ctx, None, "tp"),
        P(None, None, "tp"),
        P(None, "tp"),
        P("tp", ctx),
    )
    return jax.shard_map(
        local, mesh=paired, in_specs=placed, out_specs=P(ctx, "tp"), check_vma=False
    )
```

```python
import jax
import jax.numpy as jnp
from jax import lax
from jax.sharding import Mesh
from jax.sharding import PartitionSpec as P


def shifted(value, axis, steps):
    count = lax.axis_size(axis)
    first, last = (max(0, -steps), min(count, count - steps))
    return lax.ppermute(value, axis, [(source, source + steps) for source in range(first, last)])


def swap_pair(value):
    return lax.ppermute(value, "lo", [(0, 1), (1, 0)])


def toeplitz_pair(long_filter):
    filter_len = long_filter.shape[0]
    tap = lax.broadcasted_iota(jnp.int32, (filter_len, filter_len, filter_len), 0)
    offset = lax.broadcasted_iota(jnp.int32, (filter_len, filter_len, filter_len), 1) - (
        lax.broadcasted_iota(jnp.int32, (filter_len, filter_len, filter_len), 2)
    )
    table = long_filter.T

    def spread(hot):
        return jnp.einsum("gm,mts->gts", table, hot.astype(table.dtype))

    return (spread(offset == tap), spread(offset + filter_len == tap))


def half_of(value, axis, half):
    size = value.shape[axis] // 2
    return lax.dynamic_slice_in_dim(value, half * size, size, axis)


def pair_ordered(mine, theirs, half, axis):
    first = jnp.where(half == 0, mine, theirs)
    second = jnp.where(half == 0, theirs, mine)
    return jnp.concatenate([first, second], axis=axis)


def ring_order(count):
    return list(range(0, count, 2)) + list(range(count - 1 - count % 2, 0, -2))


def local(tokens, norm_gain, w_in, short_filter, long_filter, w_out):
    own_rows, local_width = tokens.shape
    n_tp = lax.axis_size("tp")
    n_hi = lax.axis_size("hi")
    model_width = local_width * n_tp
    short_taps = short_filter.shape[0]
    filter_len = long_filter.shape[0]
    w_rows = w_in.shape[0]
    half = lax.axis_index("lo")
    other = 1 - half
    half_width = local_width // 2

    pair_tokens = pair_ordered(tokens, swap_pair(tokens), half, 0)
    pair_tokens = lax.all_gather(pair_tokens, "tp", axis=1, tiled=True)
    row_count = pair_tokens.shape[0]
    wide_float = pair_tokens.astype(jnp.float32)
    scale = lax.rsqrt(jnp.mean(wide_float * wide_float, axis=-1, keepdims=True) + 1e-06)
    normed = (wide_float * scale * norm_gain).astype(jnp.bfloat16)

    own_piece = half_of(w_in, 2, half).reshape(w_rows, 3 * half_width)
    partner_piece = swap_pair(half_of(w_in, 2, other)).reshape(w_rows, 3 * half_width)
    order = ring_order(n_hi)
    place = [0] * n_hi
    for index, member in enumerate(order):
        place[member] = index
    order_table = jnp.array(order, jnp.int32)
    here = jnp.array(place, jnp.int32)[lax.axis_index("hi")]
    forward = [(order[i], order[(i + 1) % n_hi]) for i in range(n_hi)]
    backward = [(order[(i + 1) % n_hi], order[i]) for i in range(n_hi)]

    e_cols = w_out.shape[1]
    own_out = half_of(w_out, 0, half)
    partner_out = swap_pair(half_of(w_out, 0, other))

    n_ctx = 2 * n_hi
    gathered_w = jnp.zeros((n_ctx, w_rows, 3 * half_width), jnp.bfloat16)
    gathered_o = jnp.zeros((half_width, n_ctx, e_cols), jnp.bfloat16)

    def store(buffer, piece, ctx_index):
        return lax.dynamic_update_slice_in_dim(buffer, piece[None], ctx_index, axis=0)

    def store_out(buffer, piece, ctx_index):
        return lax.dynamic_update_slice_in_dim(buffer, piece[:, None], ctx_index, axis=1)

    current, previous = toeplitz_pair(half_of(long_filter, 1, half))
    for step in range(n_hi):
        if step > 0:
            own_piece = lax.ppermute(own_piece, "hi", forward)
            partner_piece = lax.ppermute(partner_piece, "hi", backward)
            own_out = lax.ppermute(own_out, "hi", forward)
            partner_out = lax.ppermute(partner_out, "hi", backward)
        own_at = 2 * order_table[(here - step) % n_hi] + half
        partner_at = 2 * order_table[(here + step) % n_hi] + other
        gathered_w = store(gathered_w, own_piece, own_at)
        gathered_w = store(gathered_w, partner_piece, partner_at)
        gathered_o = store_out(gathered_o, own_out, own_at)
        gathered_o = store_out(gathered_o, partner_out, partner_at)
    o_full = gathered_o.reshape(half_width, n_ctx * e_cols)

    projected = jnp.dot(
        normed,
        gathered_w.reshape(n_ctx * w_rows, 3 * half_width),
        preferred_element_type=jnp.float32,
    )
    projected = projected.astype(jnp.bfloat16).reshape(row_count, 3, half_width)

    taps = half_of(short_filter, 2, half)
    prior_rows = shifted(projected[row_count - (short_taps - 1) :], "hi", 1)
    featured = jnp.zeros((row_count,) + projected.shape[1:], jnp.float32)
    for tap in range(short_taps):
        shifted_rows = jnp.concatenate(
            [prior_rows[short_taps - 1 - tap :], projected[: row_count - tap]], axis=0
        )
        featured = featured + taps[tap] * shifted_rows.astype(jnp.float32)
    mixed = (featured[:, 1] * featured[:, 2]).astype(jnp.bfloat16)
    mixed_prior = shifted(mixed[row_count - (filter_len - 1) :], "hi", 1)
    query = featured[:, 0]
    zero_row = jnp.zeros((1, half_width), jnp.bfloat16)
    groups_here = long_filter.shape[1] // 2
    group_size = half_width // groups_here
    block_shape = (filter_len, groups_here, group_size)
    mix_blocks = mixed.reshape((row_count // filter_len,) + block_shape)
    halo_block = jnp.concatenate([zero_row, mixed_prior], axis=0).reshape((1,) + block_shape)

    def apply(table, blocks):
        return jnp.einsum("gts,bsgc->btgc", table, blocks, preferred_element_type=jnp.float32)

    filtered = apply(current, mix_blocks)
    filtered = filtered + jnp.concatenate(
        [apply(previous, halo_block), apply(previous, mix_blocks[:-1])], axis=0
    )
    gated = (query * filtered.reshape(row_count, half_width)).astype(jnp.bfloat16)

    def out_terms(rows):
        terms = jnp.dot(rows, o_full, preferred_element_type=jnp.float32).astype(jnp.bfloat16)
        return lax.psum_scatter(terms, "tp", scatter_dimension=1, tiled=True)

    arrived = swap_pair(out_terms(half_of(gated, 0, other)))
    summed = out_terms(half_of(gated, 0, half)).astype(jnp.float32) + arrived.astype(jnp.float32)
    return (tokens.astype(jnp.float32) + summed).astype(jnp.bfloat16)


def solution(mesh):
    n_ctx, n_tp = mesh.devices.shape
    paired = Mesh(mesh.devices.reshape(n_ctx // 2, 2, n_tp), ("hi", "lo", "tp"))
    ctx = ("hi", "lo")
    placed = (
        P(ctx, "tp"),
        P(),
        P(ctx, None, "tp"),
        P(None, None, "tp"),
        P(None, "tp"),
        P("tp", ctx),
    )
    return jax.shard_map(
        local, mesh=paired, in_specs=placed, out_specs=P(ctx, "tp"), check_vma=False
    )
```

```python
import jax
import jax.numpy as jnp
from jax import lax
from jax.sharding import Mesh
from jax.sharding import PartitionSpec as P


def shifted(value, axis, steps):
    count = lax.axis_size(axis)
    first, last = (max(0, -steps), min(count, count - steps))
    return lax.ppermute(value, axis, [(source, source + steps) for source in range(first, last)])


def swap_pair(value):
    return lax.ppermute(value, "lo", [(0, 1), (1, 0)])


def toeplitz_pair(long_filter):
    filter_len = long_filter.shape[0]
    tap = lax.broadcasted_iota(jnp.int32, (filter_len, filter_len, filter_len), 0)
    offset = lax.broadcasted_iota(jnp.int32, (filter_len, filter_len, filter_len), 1) - (
        lax.broadcasted_iota(jnp.int32, (filter_len, filter_len, filter_len), 2)
    )
    table = long_filter.T

    def spread(hot):
        return jnp.einsum("gm,mts->gts", table, hot.astype(table.dtype))

    return (spread(offset == tap), spread(offset + filter_len == tap))


def featurize(extended, short_filter, count):
    short_taps = short_filter.shape[0]
    ext_float = extended.astype(jnp.float32)
    featured = jnp.zeros((count,) + extended.shape[1:], jnp.float32)
    for tap in range(short_taps):
        featured = (
            featured
            + short_filter[tap] * ext_float[short_taps - 1 - tap : short_taps - 1 - tap + count]
        )
    return featured


def half_of(value, axis, half):
    size = value.shape[axis] // 2
    return lax.dynamic_slice_in_dim(value, half * size, size, axis)


def pair_ordered(mine, theirs, half, axis):
    first = jnp.where(half == 0, mine, theirs)
    second = jnp.where(half == 0, theirs, mine)
    return jnp.concatenate([first, second], axis=axis)


def ring_order(count):
    return list(range(0, count, 2)) + list(range(count - 1 - count % 2, 0, -2))


def local(tokens, norm_gain, w_in, short_filter, long_filter, w_out):
    own_rows, local_width = tokens.shape
    n_tp = lax.axis_size("tp")
    n_hi = lax.axis_size("hi")
    model_width = local_width * n_tp
    short_taps = short_filter.shape[0]
    filter_len = long_filter.shape[0]
    w_rows = w_in.shape[0]
    half = lax.axis_index("lo")
    other = 1 - half
    half_width = local_width // 2

    pair_tokens = pair_ordered(tokens, swap_pair(tokens), half, 0)
    pair_tokens = lax.all_gather(pair_tokens, "tp", axis=1, tiled=True)
    row_count = pair_tokens.shape[0]
    wide_float = pair_tokens.astype(jnp.float32)
    scale = lax.rsqrt(jnp.mean(wide_float * wide_float, axis=-1, keepdims=True) + 1e-06)
    normed = (wide_float * scale * norm_gain).astype(jnp.bfloat16)

    own_piece = half_of(w_in, 2, half).reshape(w_rows, 3 * half_width)
    partner_piece = swap_pair(half_of(w_in, 2, other)).reshape(w_rows, 3 * half_width)
    order = ring_order(n_hi)
    place = [0] * n_hi
    for index, member in enumerate(order):
        place[member] = index
    order_table = jnp.array(order, jnp.int32)
    here = jnp.array(place, jnp.int32)[lax.axis_index("hi")]
    forward = [(order[i], order[(i + 1) % n_hi]) for i in range(n_hi)]
    backward = [(order[(i + 1) % n_hi], order[i]) for i in range(n_hi)]

    e_cols = w_out.shape[1]
    own_out = half_of(w_out, 0, half)
    partner_out = swap_pair(half_of(w_out, 0, other))

    n_ctx = 2 * n_hi
    gathered_w = jnp.zeros((n_ctx, w_rows, 3 * half_width), jnp.bfloat16)
    gathered_o = jnp.zeros((half_width, n_ctx, e_cols), jnp.bfloat16)

    def store(buffer, piece, ctx_index):
        return lax.dynamic_update_slice_in_dim(buffer, piece[None], ctx_index, axis=0)

    def store_out(buffer, piece, ctx_index):
        return lax.dynamic_update_slice_in_dim(buffer, piece[:, None], ctx_index, axis=1)

    current, previous = toeplitz_pair(half_of(long_filter, 1, half))
    for step in range(n_hi):
        if step > 0:
            own_piece = lax.ppermute(own_piece, "hi", forward)
            partner_piece = lax.ppermute(partner_piece, "hi", backward)
            own_out = lax.ppermute(own_out, "hi", forward)
            partner_out = lax.ppermute(partner_out, "hi", backward)
        own_at = 2 * order_table[(here - step) % n_hi] + half
        partner_at = 2 * order_table[(here + step) % n_hi] + other
        gathered_w = store(gathered_w, own_piece, own_at)
        gathered_w = store(gathered_w, partner_piece, partner_at)
        gathered_o = store_out(gathered_o, own_out, own_at)
        gathered_o = store_out(gathered_o, partner_out, partner_at)
    o_full = gathered_o.reshape(half_width, n_ctx * e_cols)

    projected = jnp.einsum(
        "td,dkc->tkc",
        normed,
        gathered_w.reshape(n_ctx * w_rows, 3, half_width),
        preferred_element_type=jnp.float32,
    ).astype(jnp.bfloat16)

    taps = half_of(short_filter, 2, half)
    prior_rows = shifted(projected[row_count - (short_taps - 1) :], "hi", 1)
    featured = featurize(jnp.concatenate([prior_rows, projected], axis=0), taps, row_count)
    mixed = (featured[:, 1] * featured[:, 2]).astype(jnp.bfloat16)
    mixed_prior = shifted(mixed[row_count - (filter_len - 1) :], "hi", 1)
    query = featured[:, 0]
    zero_row = jnp.zeros((1, half_width), jnp.bfloat16)
    groups_here = long_filter.shape[1] // 2
    group_size = half_width // groups_here
    block_shape = (filter_len, groups_here, group_size)
    mix_blocks = mixed.reshape((row_count // filter_len,) + block_shape)
    halo_block = jnp.concatenate([zero_row, mixed_prior], axis=0).reshape((1,) + block_shape)

    def apply(table, blocks):
        return jnp.einsum("gts,bsgc->btgc", table, blocks, preferred_element_type=jnp.float32)

    filtered = apply(current, mix_blocks)
    filtered = filtered + jnp.concatenate(
        [apply(previous, halo_block), apply(previous, mix_blocks[:-1])], axis=0
    )
    gated = (query * filtered.reshape(row_count, half_width)).astype(jnp.bfloat16)

    def out_terms(rows):
        terms = jnp.dot(rows, o_full, preferred_element_type=jnp.float32).astype(jnp.bfloat16)
        return lax.psum_scatter(terms, "tp", scatter_dimension=1, tiled=True)

    arrived = swap_pair(out_terms(half_of(gated, 0, other)))
    summed = out_terms(half_of(gated, 0, half)).astype(jnp.float32) + arrived.astype(jnp.float32)
    return (tokens.astype(jnp.float32) + summed).astype(jnp.bfloat16)


def solution(mesh):
    n_ctx, n_tp = mesh.devices.shape
    paired = Mesh(mesh.devices.reshape(n_ctx // 2, 2, n_tp), ("hi", "lo", "tp"))
    ctx = ("hi", "lo")
    placed = (
        P(ctx, "tp"),
        P(),
        P(ctx, None, "tp"),
        P(None, None, "tp"),
        P(None, "tp"),
        P("tp", ctx),
    )
    return jax.shard_map(
        local, mesh=paired, in_specs=placed, out_specs=P(ctx, "tp"), check_vma=False
    )
```
